512 devices in a mesh: atoms: 32 (over x_hi, z, core), loops: 16 (over x_lo, y).
Axes of the slice: x: 4 (x_hi: 2, x_lo: 2; x = x_hi * 2 + x_lo), y: 8, z: 8, core: 2. Of those that a mesh axis runs over, the one named last changes fastest.
Arguments:
- atom_site: int32 [131072], P('atoms'), may hold values from 0 to 262143, as said below
- loop_cells: int32 [3, 4096], P(None, 'loops'), may hold values from -200 to 199
- loop_burgers: int32 [4096], P('loops'), may hold values from 0 to 3
- loop_habit: int32 [4096], P('loops'), may hold values from 0 to 5
- loop_radius: float32 [4096], P('loops'), may hold values from 10 to 40
Outputs:
- log_intensity: float32 [64, 128, 128], P('loops', 'atoms')
The draws below stay inside these ranges and needn't reach their ends.
Inputs may be any that keep to these rules, and one draw needn't show every extreme that they name: `atom_site`: site numbers are distinct; the first and the last site of the window are always occupied.
All inputs are finite; a program needn't handle non-finite values.
Results may differ from the reference program's by a relative error of at most 0.0003.
Values sent between devices are 32-bit elements; how exact they have to be, the bound alone decides.
No kernel may reach another device: no remote copies, remote signals or barrier semaphores. Data moves between devices by JAX's collectives and lax.ppermute only.
A program may use at most 64 MiB of HBM per device.

```python
import math
import jax
import jax.numpy as jnp
import numpy as np
from jax import lax

WIN_X = 32
WIN_Y = 32
LOOP_REACH = 200
QX = 128
QY = 128
QZ = 64
ATOMS = 131072
LOOPS = 4096


def draw_atom_site(key, part):
    inner = jax.random.permutation(key, 2 * ATOMS - 2)[:ATOMS - 2].astype(jnp.int32) + 1
    first = jnp.zeros((1,), jnp.int32)
    last = jnp.full((1,), 2 * ATOMS - 1, jnp.int32)
    return jnp.concatenate([first, inner, last]).astype(jnp.int32)


def plant(entries, own_key, smallest, high):
    spot = [jax.random.randint(jax.random.fold_in(own_key, axis), (), 0, length) for axis, length in enumerate(entries.shape)]
    widest = entries.shape.index(max(entries.shape))
    beside = spot[:widest] + [(spot[widest] + 1) % entries.shape[widest]] + spot[widest + 1:]
    return entries.at[tuple(spot)].set(smallest).at[tuple(beside)].set(high)


def steps_of(stream_key, shape, shards, smallest, high):
    factor_of = 1.0
    for dim, parts in shards:
        steps = jax.random.uniform(jax.random.fold_in(jax.random.fold_in(stream_key, 6), dim), (parts,), jnp.float32, smallest / len(shards), high / len(shards))
        factor_of = factor_of * jnp.repeat(jnp.exp(steps), shape[dim] // parts).reshape((-1,) + (1,) * (len(shape) - 1 - dim))
    return factor_of


def setup_inputs(seed: int = 0) -> dict:
    arg_keys = jax.random.split(jax.random.key(seed), 6)
    return {
        "atom_site": draw_atom_site(jax.random.fold_in(arg_keys[5], 71), 0),
        "loop_cells": plant(jax.random.randint(arg_keys[1], (3, LOOPS), 0 - LOOP_REACH, LOOP_REACH), jax.random.fold_in(arg_keys[1], 1), 0 - LOOP_REACH, LOOP_REACH - 1).astype(jnp.int32),
        "loop_burgers": plant(jax.random.randint(arg_keys[2], (LOOPS,), 0, 4), jax.random.fold_in(arg_keys[2], 1), 0, 3).astype(jnp.int32),
        "loop_habit": plant(jax.random.randint(arg_keys[3], (LOOPS,), 0, 6), jax.random.fold_in(arg_keys[3], 1), 0, 5).astype(jnp.int32),
        "loop_radius": jnp.clip(jnp.exp(math.log(40.0) - 1.3862944 * jax.random.uniform(arg_keys[4], (LOOPS,), jnp.float32) ** steps_of(arg_keys[4], (LOOPS,), ((0, 16),), -0.2, 0.2)), 10.0, 40.0),
    }


LATTICE = 2.8665
POISSON = 0.29
TWO_PI = 2.0 * math.pi
BURGERS_TABLE = np.array([[1.0, 1.0, 1.0], [-1.0, 1.0, 1.0], [1.0, -1.0, 1.0], [1.0, 1.0, -1.0]]) * (0.5 * LATTICE)
NORMAL_TABLE = np.array([[1.0, 1.0, 0.0], [1.0, -1.0, 0.0], [1.0, 0.0, 1.0], [1.0, 0.0, -1.0], [0.0, 1.0, 1.0], [0.0, 1.0, -1.0]]) * 0.70710678

def lookup(index, table):
    columns = []
    for column in range(3):
        total = jnp.zeros(index.shape, jnp.float32)
        for entry in range(table.shape[0]):
            total = total + jnp.where(index == entry, jnp.float32(table[entry, column]), jnp.float32(0.0))
        columns.append(total)
    return jnp.stack(columns)

def site_anchor(site):
    basis = site % 2
    cell = site // 2
    first = cell % WIN_X
    second = cell // WIN_X % WIN_Y
    third = cell // (WIN_X * WIN_Y)
    cells = jnp.stack([first, second, third]).astype(jnp.float32)
    return LATTICE * (cells + 0.5 * basis.astype(jnp.float32)[None, :])

def loop_centre(cells):
    return LATTICE * (cells.astype(jnp.float32) + 0.25)

def loop_field(anchor, centre, burgers, normal, radius):
    offset = anchor[:, None, :] - centre[:, :, None]
    radius_sq = (radius * radius)[:, None]
    distance_sq = lax.optimization_barrier(jnp.sum(offset * offset, axis=0)) + radius_sq
    unit_dir = offset * lax.rsqrt(distance_sq)[None]
    along_b = lax.optimization_barrier(jnp.sum(burgers[:, :, None] * unit_dir, axis=0))
    along_n = lax.optimization_barrier(jnp.sum(normal[:, :, None] * unit_dir, axis=0))
    burgers_normal = lax.optimization_barrier(jnp.sum(burgers * normal, axis=0))[:, None]
    strength = radius_sq / (8.0 * (1.0 - POISSON) * distance_sq)
    field = (1.0 - 2.0 * POISSON) * (burgers[:, :, None] * along_n[None] + normal[:, :, None] * along_b[None])
    field = field - burgers_normal[None] * unit_dir + 3.0 * unit_dir * (along_b * along_n)[None]
    return lax.optimization_barrier(jnp.sum(strength[None] * field, axis=1))

def waves(first, count, total, centre):
    steps = first + jnp.arange(count, dtype=jnp.float32)
    return TWO_PI / LATTICE * (centre + (steps - total * 0.5 + 0.5) / QX)

def factor_block(xcosines, xsines, zcosines, zsines, ytable):
    ywidth = ytable.shape[1] // 2
    left_real = zcosines[None, :, :] * xcosines[:, None, :] - zsines[None, :, :] * xsines[:, None, :]
    left_imag = zcosines[None, :, :] * xsines[:, None, :] + zsines[None, :, :] * xcosines[:, None, :]
    left_pair = jnp.stack([left_real, left_imag], axis=2)
    product = jnp.einsum('xzca,ad->xzcd', left_pair, ytable, precision=lax.Precision.HIGHEST, preferred_element_type=jnp.float32)
    real_part = product[:, :, 0, :ywidth] - product[:, :, 1, ywidth:]
    imag_part = product[:, :, 0, ywidth:] + product[:, :, 1, :ywidth]
    return jnp.stack([real_part, imag_part], axis=1)

def reference(atom_site, loop_cells, loop_burgers, loop_habit, loop_radius):
    anchor = site_anchor(atom_site)
    centre = loop_centre(loop_cells)
    burgers = lookup(loop_burgers, BURGERS_TABLE)
    normal = lookup(loop_habit, NORMAL_TABLE)
    loop_total = centre.shape[1]
    block_size = math.gcd(loop_total, 128)

    def add_block(number, running):
        begin = (number * block_size).astype(jnp.int32)
        return running + loop_field(anchor, lax.dynamic_slice_in_dim(centre, begin, block_size, 1), lax.dynamic_slice_in_dim(burgers, begin, block_size, 1), lax.dynamic_slice_in_dim(normal, begin, block_size, 1), lax.dynamic_slice_in_dim(loop_radius, begin, block_size, 0))
    displacement = lax.fori_loop(0, loop_total // block_size, add_block, jnp.zeros(anchor.shape, jnp.float32))
    position = anchor + displacement
    atom_total = position.shape[1]
    xwaves = waves(jnp.float32(0.0), QX, QX, 1.0)
    ywaves = waves(jnp.float32(0.0), QY, QY, 1.0)
    zwaves = waves(jnp.float32(0.0), QZ, QZ, 0.0)
    xangle = xwaves[:, None] * position[0][None, :]
    yangle = position[1][:, None] * ywaves[None, :]
    zangle = zwaves[:, None] * position[2][None, :]
    xcosines, xsines = (jnp.cos(xangle), jnp.sin(xangle))
    zcosines, zsines = (jnp.cos(zangle), jnp.sin(zangle))
    ytable = jnp.concatenate([jnp.cos(yangle), jnp.sin(yangle)], axis=1)

    def one_plane(plane):
        zc = lax.dynamic_slice_in_dim(zcosines, plane, 1, 0)
        zs = lax.dynamic_slice_in_dim(zsines, plane, 1, 0)
        return factor_block(xcosines, xsines, zc, zs, ytable)[:, :, 0, :]
    amplitude = lax.map(one_plane, jnp.arange(QZ, dtype=jnp.int32))
    power = amplitude[:, :, 0, :] ** 2 + amplitude[:, :, 1, :] ** 2
    return jnp.log1p(power / atom_total)
```

```python
import math

import jax
import jax.numpy as jnp
import numpy as np
from jax import lax
from jax.sharding import PartitionSpec as P

WIN_X = 32
WIN_Y = 32
QX = 128
QY = 128
QZ = 64


LATTICE = 2.8665
POISSON = 0.29
TWO_PI = 2.0 * math.pi
BURGERS_TABLE = np.array(
    [[1.0, 1.0, 1.0], [-1.0, 1.0, 1.0], [1.0, -1.0, 1.0], [1.0, 1.0, -1.0]]
) * (0.5 * LATTICE)
NORMAL_TABLE = (
    np.array(
        [
            [1.0, 1.0, 0.0],
            [1.0, -1.0, 0.0],
            [1.0, 0.0, 1.0],
            [1.0, 0.0, -1.0],
            [0.0, 1.0, 1.0],
            [0.0, 1.0, -1.0],
        ]
    )
    * 0.70710678
)


def lookup(index, table):
    columns = []
    for column in range(3):
        total = jnp.zeros(index.shape, jnp.float32)
        for entry in range(table.shape[0]):
            total = total + jnp.where(
                index == entry, jnp.float32(table[entry, column]), jnp.float32(0.0)
            )
        columns.append(total)
    return jnp.stack(columns)


def site_anchor(site):
    basis = site % 2
    cell = site // 2
    first = cell % WIN_X
    second = cell // WIN_X % WIN_Y
    third = cell // (WIN_X * WIN_Y)
    cells = jnp.stack([first, second, third]).astype(jnp.float32)
    return LATTICE * (cells + 0.5 * basis.astype(jnp.float32)[None, :])


def loop_centre(cells):
    return LATTICE * (cells.astype(jnp.float32) + 0.25)


def loop_field(anchor, centre, burgers, normal, radius):
    offset = anchor[:, None, :] - centre[:, :, None]
    radius_sq = (radius * radius)[:, None]
    distance_sq = jnp.sum(offset * offset, axis=0) + radius_sq
    unit_dir = offset * lax.rsqrt(distance_sq)[None]
    along_b = jnp.sum(burgers[:, :, None] * unit_dir, axis=0)
    along_n = jnp.sum(normal[:, :, None] * unit_dir, axis=0)
    burgers_normal = jnp.sum(burgers * normal, axis=0)[:, None]
    strength = radius_sq / (8.0 * (1.0 - POISSON) * distance_sq)
    field = (1.0 - 2.0 * POISSON) * (
        burgers[:, :, None] * along_n[None] + normal[:, :, None] * along_b[None]
    )
    field = field - burgers_normal[None] * unit_dir + 3.0 * unit_dir * (along_b * along_n)[None]
    return jnp.sum(strength[None] * field, axis=1)


def waves(first, count, total, centre):
    steps = first + jnp.arange(count, dtype=jnp.float32)
    return TWO_PI / LATTICE * (centre + (steps - total * 0.5 + 0.5) / QX)


def factor_block(xcosines, xsines, zcosines, zsines, ytable):
    ywidth = ytable.shape[1] // 2
    left_real = (
        zcosines[None, :, :] * xcosines[:, None, :] - zsines[None, :, :] * xsines[:, None, :]
    )
    left_imag = (
        zcosines[None, :, :] * xsines[:, None, :] + zsines[None, :, :] * xcosines[:, None, :]
    )
    left_pair = jnp.stack([left_real, left_imag], axis=2)
    product = jnp.einsum(
        "xzca,ad->xzcd",
        left_pair,
        ytable,
        precision=lax.Precision.HIGHEST,
        preferred_element_type=jnp.float32,
    )
    real_part = product[:, :, 0, :ywidth] - product[:, :, 1, ywidth:]
    imag_part = product[:, :, 0, ywidth:] + product[:, :, 1, :ywidth]
    return jnp.stack([real_part, imag_part], axis=1)


def phase_tables(position, xwaves, ywaves, zwaves):
    xangle = xwaves[:, None] * position[0][None, :]
    yangle = position[1][:, None] * ywaves[None, :]
    zangle = zwaves[:, None] * position[2][None, :]
    ytable = jnp.concatenate([jnp.cos(yangle), jnp.sin(yangle)], axis=1)
    return (jnp.cos(xangle), jnp.sin(xangle), jnp.cos(zangle), jnp.sin(zangle), ytable)


def body(atom_site, loop_cells, loop_burgers, loop_habit, loop_radius):
    anchor = site_anchor(atom_site)
    centre = loop_centre(loop_cells)
    burgers = lookup(loop_burgers, BURGERS_TABLE)
    normal = lookup(loop_habit, NORMAL_TABLE)
    loop_count = centre.shape[1]
    block_size = math.gcd(loop_count, 64)

    def add_block(number, running):
        begin = number * block_size
        return running + loop_field(
            anchor,
            lax.dynamic_slice_in_dim(centre, begin, block_size, 1),
            lax.dynamic_slice_in_dim(burgers, begin, block_size, 1),
            lax.dynamic_slice_in_dim(normal, begin, block_size, 1),
            lax.dynamic_slice_in_dim(loop_radius, begin, block_size, 0),
        )

    partial_field = lax.fori_loop(
        0, loop_count // block_size, add_block, jnp.zeros(anchor.shape, jnp.float32)
    )
    loop_groups = lax.axis_size("loops")
    chunk = partial_field.shape[1] // loop_groups
    owned = lax.all_to_all(
        partial_field.reshape(3, loop_groups, chunk), "loops", 1, 1, tiled=True
    ).sum(axis=1)
    displacement = lax.all_to_all(
        jnp.broadcast_to(owned[:, None], (3, loop_groups, chunk)), "loops", 1, 1, tiled=True
    ).reshape(3, -1)
    position = anchor + displacement
    group_count = lax.axis_size("atoms")
    zrows = QZ // lax.axis_size("loops")
    atom_total = position.shape[1] * group_count
    zfirst = (lax.axis_index("loops") * zrows).astype(jnp.float32)
    zwaves = waves(zfirst, zrows, QZ, 0.0)
    ywaves = waves(jnp.float32(0.0), QY, QY, 1.0)
    xwaves = waves(jnp.float32(0.0), QX, QX, 1.0)
    xcosines, xsines, zcosines, zsines, ytable = phase_tables(position, xwaves, ywaves, zwaves)
    partial = factor_block(xcosines, xsines, zcosines, zsines, ytable)
    blocks = partial.reshape(group_count, -1, *partial.shape[1:])
    summed = lax.all_to_all(blocks, "atoms", 0, 0, tiled=True).sum(axis=0)
    power = summed[:, 0] ** 2 + summed[:, 1] ** 2
    return jnp.log1p(jnp.transpose(power, (1, 0, 2)) / atom_total)


def solution(mesh):
    placed = (P("atoms"), P(None, "loops"), P("loops"), P("loops"), P("loops"))
    return jax.shard_map(
        body, mesh=mesh, in_specs=placed, out_specs=P("loops", "atoms", None), check_vma=False
    )
```

```python
import math

import jax
import jax.numpy as jnp
import numpy as np
from jax import lax
from jax.sharding import PartitionSpec as P

WIN_X = 32
WIN_Y = 32
QX = 128
QY = 128
QZ = 64


LATTICE = 2.8665
POISSON = 0.29
TWO_PI = 2.0 * math.pi
BURGERS_TABLE = np.array(
    [[1.0, 1.0, 1.0], [-1.0, 1.0, 1.0], [1.0, -1.0, 1.0], [1.0, 1.0, -1.0]]
) * (0.5 * LATTICE)
NORMAL_TABLE = (
    np.array(
        [
            [1.0, 1.0, 0.0],
            [1.0, -1.0, 0.0],
            [1.0, 0.0, 1.0],
            [1.0, 0.0, -1.0],
            [0.0, 1.0, 1.0],
            [0.0, 1.0, -1.0],
        ]
    )
    * 0.70710678
)


def lookup(index, table):
    columns = []
    for column in range(3):
        total = jnp.zeros(index.shape, jnp.float32)
        for entry in range(table.shape[0]):
            total = total + jnp.where(
                index == entry, jnp.float32(table[entry, column]), jnp.float32(0.0)
            )
        columns.append(total)
    return jnp.stack(columns)


def site_anchor(site):
    basis = site % 2
    cell = site // 2
    first = cell % WIN_X
    second = cell // WIN_X % WIN_Y
    third = cell // (WIN_X * WIN_Y)
    cells = jnp.stack([first, second, third]).astype(jnp.float32)
    return LATTICE * (cells + 0.5 * basis.astype(jnp.float32)[None, :])


def loop_centre(cells):
    return LATTICE * (cells.astype(jnp.float32) + 0.25)


def loop_field(anchor, centre, burgers, normal, radius):
    offset = anchor[:, None, :] - centre[:, :, None]
    radius_sq = (radius * radius)[:, None]
    distance_sq = jnp.sum(offset * offset, axis=0) + radius_sq
    unit_dir = offset * lax.rsqrt(distance_sq)[None]
    along_b = jnp.sum(burgers[:, :, None] * unit_dir, axis=0)
    along_n = jnp.sum(normal[:, :, None] * unit_dir, axis=0)
    burgers_normal = jnp.sum(burgers * normal, axis=0)[:, None]
    strength = radius_sq / (8.0 * (1.0 - POISSON) * distance_sq)
    field = (1.0 - 2.0 * POISSON) * (
        burgers[:, :, None] * along_n[None] + normal[:, :, None] * along_b[None]
    )
    field = field - burgers_normal[None] * unit_dir + 3.0 * unit_dir * (along_b * along_n)[None]
    return jnp.sum(strength[None] * field, axis=1)


def waves(first, count, total, centre):
    steps = first + jnp.arange(count, dtype=jnp.float32)
    return TWO_PI / LATTICE * (centre + (steps - total * 0.5 + 0.5) / QX)


def factor_block(xcosines, xsines, zcosines, zsines, ytable):
    ywidth = ytable.shape[1] // 2
    left_real = (
        zcosines[None, :, :] * xcosines[:, None, :] - zsines[None, :, :] * xsines[:, None, :]
    )
    left_imag = (
        zcosines[None, :, :] * xsines[:, None, :] + zsines[None, :, :] * xcosines[:, None, :]
    )
    left_pair = jnp.stack([left_real, left_imag], axis=2)
    product = jnp.einsum(
        "xzca,ad->xzcd",
        left_pair,
        ytable,
        precision=lax.Precision.HIGH,
        preferred_element_type=jnp.float32,
    )
    real_part = product[:, :, 0, :ywidth] - product[:, :, 1, ywidth:]
    imag_part = product[:, :, 0, ywidth:] + product[:, :, 1, :ywidth]
    return jnp.stack([real_part, imag_part], axis=1)


def phase_tables(position, xwaves, ywaves, zwaves):
    xangle = xwaves[:, None] * position[0][None, :]
    yangle = position[1][:, None] * ywaves[None, :]
    zangle = zwaves[:, None] * position[2][None, :]
    ytable = jnp.concatenate([jnp.cos(yangle), jnp.sin(yangle)], axis=1)
    return (jnp.cos(xangle), jnp.sin(xangle), jnp.cos(zangle), jnp.sin(zangle), ytable)


def body(atom_site, loop_cells, loop_burgers, loop_habit, loop_radius):
    anchor = site_anchor(atom_site)
    centre = loop_centre(loop_cells)
    burgers = lookup(loop_burgers, BURGERS_TABLE)
    normal = lookup(loop_habit, NORMAL_TABLE)
    loop_count = centre.shape[1]
    block_size = math.gcd(loop_count, 64)

    def add_block(number, running):
        begin = number * block_size
        return running + loop_field(
            anchor,
            lax.dynamic_slice_in_dim(centre, begin, block_size, 1),
            lax.dynamic_slice_in_dim(burgers, begin, block_size, 1),
            lax.dynamic_slice_in_dim(normal, begin, block_size, 1),
            lax.dynamic_slice_in_dim(loop_radius, begin, block_size, 0),
        )

    partial_field = lax.fori_loop(
        0, loop_count // block_size, add_block, jnp.zeros(anchor.shape, jnp.float32)
    )
    loop_groups = lax.axis_size("loops")
    chunk = partial_field.shape[1] // loop_groups
    owned = lax.all_to_all(
        partial_field.reshape(3, loop_groups, chunk), "loops", 1, 1, tiled=True
    ).sum(axis=1)
    displacement = lax.all_to_all(
        jnp.broadcast_to(owned[:, None], (3, loop_groups, chunk)), "loops", 1, 1, tiled=True
    ).reshape(3, -1)
    position = anchor + displacement
    group_count = lax.axis_size("atoms")
    zrows = QZ // lax.axis_size("loops")
    atom_total = position.shape[1] * group_count
    zfirst = (lax.axis_index("loops") * zrows).astype(jnp.float32)
    zwaves = waves(zfirst, zrows, QZ, 0.0)
    ywaves = waves(jnp.float32(0.0), QY, QY, 1.0)
    xwaves = waves(jnp.float32(0.0), QX, QX, 1.0)
    xcosines, xsines, zcosines, zsines, ytable = phase_tables(position, xwaves, ywaves, zwaves)
    partial = factor_block(xcosines, xsines, zcosines, zsines, ytable)
    blocks = partial.reshape(group_count, -1, *partial.shape[1:])
    summed = lax.all_to_all(blocks, "atoms", 0, 0, tiled=True).sum(axis=0)
    power = summed[:, 0] ** 2 + summed[:, 1] ** 2
    return jnp.log1p(jnp.transpose(power, (1, 0, 2)) / atom_total)


def solution(mesh):
    placed = (P("atoms"), P(None, "loops"), P("loops"), P("loops"), P("loops"))
    return jax.shard_map(
        body, mesh=mesh, in_specs=placed, out_specs=P("loops", "atoms", None), check_vma=False
    )
```

```python
import math

import jax
import jax.numpy as jnp
import numpy as np
from jax import lax
from jax.experimental import pallas as pl
from jax.experimental.pallas import tpu as pltpu
from jax.sharding import PartitionSpec as P

WIN_X = 32
WIN_Y = 32
QX = 128
QY = 128
QZ = 64


LATTICE = 2.8665
POISSON = 0.29
TWO_PI = 2.0 * math.pi
BURGERS_TABLE = np.array(
    [[1.0, 1.0, 1.0], [-1.0, 1.0, 1.0], [1.0, -1.0, 1.0], [1.0, 1.0, -1.0]]
) * (0.5 * LATTICE)
NORMAL_TABLE = (
    np.array(
        [
            [1.0, 1.0, 0.0],
            [1.0, -1.0, 0.0],
            [1.0, 0.0, 1.0],
            [1.0, 0.0, -1.0],
            [0.0, 1.0, 1.0],
            [0.0, 1.0, -1.0],
        ]
    )
    * 0.70710678
)


def lookup(index, table):
    columns = []
    for column in range(3):
        total = jnp.zeros(index.shape, jnp.float32)
        for entry in range(table.shape[0]):
            total = total + jnp.where(
                index == entry, jnp.float32(table[entry, column]), jnp.float32(0.0)
            )
        columns.append(total)
    return jnp.stack(columns)


def site_anchor(site):
    basis = site % 2
    cell = site // 2
    first = cell % WIN_X
    second = cell // WIN_X % WIN_Y
    third = cell // (WIN_X * WIN_Y)
    cells = jnp.stack([first, second, third]).astype(jnp.float32)
    return LATTICE * (cells + 0.5 * basis.astype(jnp.float32)[None, :])


def loop_centre(cells):
    return LATTICE * (cells.astype(jnp.float32) + 0.25)


def loop_field(anchor, centre, burgers, normal, radius):
    offset = anchor[:, None, :] - centre[:, :, None]
    radius_sq = (radius * radius)[:, None]
    distance_sq = jnp.sum(offset * offset, axis=0) + radius_sq
    unit_dir = offset * lax.rsqrt(distance_sq)[None]
    along_b = jnp.sum(burgers[:, :, None] * unit_dir, axis=0)
    along_n = jnp.sum(normal[:, :, None] * unit_dir, axis=0)
    burgers_normal = jnp.sum(burgers * normal, axis=0)[:, None]
    strength = radius_sq / (8.0 * (1.0 - POISSON) * distance_sq)
    field = (1.0 - 2.0 * POISSON) * (
        burgers[:, :, None] * along_n[None] + normal[:, :, None] * along_b[None]
    )
    field = field - burgers_normal[None] * unit_dir + 3.0 * unit_dir * (along_b * along_n)[None]
    return jnp.sum(strength[None] * field, axis=1)


def waves(first, count, total, centre):
    steps = first + jnp.arange(count, dtype=jnp.float32)
    return TWO_PI / LATTICE * (centre + (steps - total * 0.5 + 0.5) / QX)


def factor_block(xcosines, xsines, zcosines, zsines, ytable):
    ywidth = ytable.shape[1] // 2
    left_real = (
        zcosines[None, :, :] * xcosines[:, None, :] - zsines[None, :, :] * xsines[:, None, :]
    )
    left_imag = (
        zcosines[None, :, :] * xsines[:, None, :] + zsines[None, :, :] * xcosines[:, None, :]
    )
    left_pair = jnp.stack([left_real, left_imag], axis=2)
    product = jnp.einsum(
        "xzca,ad->xzcd",
        left_pair,
        ytable,
        precision=lax.Precision.HIGH,
        preferred_element_type=jnp.float32,
    )
    real_part = product[:, :, 0, :ywidth] - product[:, :, 1, ywidth:]
    imag_part = product[:, :, 0, ywidth:] + product[:, :, 1, :ywidth]
    return jnp.stack([real_part, imag_part], axis=1)


def phase_tables(position, xwaves, ywaves, zwaves):
    xangle = xwaves[:, None] * position[0][None, :]
    yangle = position[1][:, None] * ywaves[None, :]
    zangle = zwaves[:, None] * position[2][None, :]
    ytable = jnp.concatenate([jnp.cos(yangle), jnp.sin(yangle)], axis=1)
    return (jnp.cos(xangle), jnp.sin(xangle), jnp.cos(zangle), jnp.sin(zangle), ytable)


FIELD_ROWS = 16


def field_kernel(table, anchor, out):
    ax, ay, az = anchor[0], anchor[1], anchor[2]

    def one_loop(number, running):
        cx, cy, cz = table[0, number], table[1, number], table[2, number]
        bx, by, bz = table[3, number], table[4, number], table[5, number]
        nx, ny, nz = table[6, number], table[7, number], table[8, number]
        radius_sq, scale, burgers_normal = table[9, number], table[10, number], table[11, number]
        dx, dy, dz = ax - cx, ay - cy, az - cz
        distance_sq = dx * dx + dy * dy + dz * dz + radius_sq
        inverse = lax.rsqrt(distance_sq)
        ux, uy, uz = dx * inverse, dy * inverse, dz * inverse
        along_b = bx * ux + by * uy + bz * uz
        along_n = nx * ux + ny * uy + nz * uz
        strength = scale * (inverse * inverse)
        mixed = 3.0 * (along_b * along_n) - burgers_normal
        fx, fy, fz = running
        gx = (1.0 - 2.0 * POISSON) * (bx * along_n + nx * along_b) + ux * mixed
        gy = (1.0 - 2.0 * POISSON) * (by * along_n + ny * along_b) + uy * mixed
        gz = (1.0 - 2.0 * POISSON) * (bz * along_n + nz * along_b) + uz * mixed
        return (fx + strength * gx, fy + strength * gy, fz + strength * gz)

    zero = jnp.zeros(ax.shape, jnp.float32)
    fx, fy, fz = lax.fori_loop(0, table.shape[1], one_loop, (zero, zero, zero), unroll=4)
    out[0] = fx
    out[1] = fy
    out[2] = fz


def partial_field(anchor, centre, burgers, normal, radius):
    atoms = anchor.shape[1]
    loops = centre.shape[1]
    radius_sq = radius * radius
    scale = radius_sq / (8.0 * (1.0 - POISSON))
    burgers_normal = jnp.sum(burgers * normal, axis=0)
    table = jnp.concatenate(
        [centre, burgers, normal, radius_sq[None], scale[None], burgers_normal[None]], axis=0
    )
    rows = atoms // 128
    tiled = anchor.reshape(3, rows, 128)
    spec = pl.BlockSpec((3, FIELD_ROWS, 128), lambda i: (0, i, 0))
    field = pl.pallas_call(
        field_kernel,
        grid=(rows // FIELD_ROWS,),
        in_specs=[pl.BlockSpec(memory_space=pltpu.SMEM), spec],
        out_specs=spec,
        out_shape=jax.ShapeDtypeStruct(tiled.shape, jnp.float32),
        cost_estimate=pl.CostEstimate(
            flops=55 * atoms * loops, transcendentals=atoms * loops, bytes_accessed=24 * atoms
        ),
    )(table, tiled)
    return field.reshape(3, atoms)


def body(atom_site, loop_cells, loop_burgers, loop_habit, loop_radius):
    anchor = site_anchor(atom_site)
    centre = loop_centre(loop_cells)
    burgers = lookup(loop_burgers, BURGERS_TABLE)
    normal = lookup(loop_habit, NORMAL_TABLE)
    partial_field_value = partial_field(anchor, centre, burgers, normal, loop_radius)
    loop_groups = lax.axis_size("loops")
    chunk = partial_field_value.shape[1] // loop_groups
    owned = lax.all_to_all(
        partial_field_value.reshape(3, loop_groups, chunk), "loops", 1, 1, tiled=True
    ).sum(axis=1)
    displacement = lax.all_to_all(
        jnp.broadcast_to(owned[:, None], (3, loop_groups, chunk)), "loops", 1, 1, tiled=True
    ).reshape(3, -1)
    position = anchor + displacement
    group_count = lax.axis_size("atoms")
    zrows = QZ // lax.axis_size("loops")
    atom_total = position.shape[1] * group_count
    zfirst = (lax.axis_index("loops") * zrows).astype(jnp.float32)
    zwaves = waves(zfirst, zrows, QZ, 0.0)
    ywaves = waves(jnp.float32(0.0), QY, QY, 1.0)
    xwaves = waves(jnp.float32(0.0), QX, QX, 1.0)
    xcosines, xsines, zcosines, zsines, ytable = phase_tables(position, xwaves, ywaves, zwaves)
    partial = factor_block(xcosines, xsines, zcosines, zsines, ytable)
    blocks = partial.reshape(group_count, -1, *partial.shape[1:])
    summed = lax.all_to_all(blocks, "atoms", 0, 0, tiled=True).sum(axis=0)
    power = summed[:, 0] ** 2 + summed[:, 1] ** 2
    return jnp.log1p(jnp.transpose(power, (1, 0, 2)) / atom_total)


def solution(mesh):
    placed = (P("atoms"), P(None, "loops"), P("loops"), P("loops"), P("loops"))
    return jax.shard_map(
        body, mesh=mesh, in_specs=placed, out_specs=P("loops", "atoms", None), check_vma=False
    )
```

```python
import math

import jax
import jax.numpy as jnp
import numpy as np
from jax import lax
from jax.experimental import pallas as pl
from jax.experimental.pallas import tpu as pltpu
from jax.sharding import PartitionSpec as P

WIN_X = 32
WIN_Y = 32
QX = 128
QY = 128
QZ = 64


LATTICE = 2.8665
POISSON = 0.29
TWO_PI = 2.0 * math.pi
BURGERS_TABLE = np.array(
    [[1.0, 1.0, 1.0], [-1.0, 1.0, 1.0], [1.0, -1.0, 1.0], [1.0, 1.0, -1.0]]
) * (0.5 * LATTICE)
NORMAL_TABLE = (
    np.array(
        [
            [1.0, 1.0, 0.0],
            [1.0, -1.0, 0.0],
            [1.0, 0.0, 1.0],
            [1.0, 0.0, -1.0],
            [0.0, 1.0, 1.0],
            [0.0, 1.0, -1.0],
        ]
    )
    * 0.70710678
)


def lookup(index, table):
    columns = []
    for column in range(3):
        total = jnp.zeros(index.shape, jnp.float32)
        for entry in range(table.shape[0]):
            total = total + jnp.where(
                index == entry, jnp.float32(table[entry, column]), jnp.float32(0.0)
            )
        columns.append(total)
    return jnp.stack(columns)


def site_anchor(site):
    basis = site % 2
    cell = site // 2
    first = cell % WIN_X
    second = cell // WIN_X % WIN_Y
    third = cell // (WIN_X * WIN_Y)
    cells = jnp.stack([first, second, third]).astype(jnp.float32)
    return LATTICE * (cells + 0.5 * basis.astype(jnp.float32)[None, :])


def loop_centre(cells):
    return LATTICE * (cells.astype(jnp.float32) + 0.25)


def loop_field(anchor, centre, burgers, normal, radius):
    offset = anchor[:, None, :] - centre[:, :, None]
    radius_sq = (radius * radius)[:, None]
    distance_sq = jnp.sum(offset * offset, axis=0) + radius_sq
    unit_dir = offset * lax.rsqrt(distance_sq)[None]
    along_b = jnp.sum(burgers[:, :, None] * unit_dir, axis=0)
    along_n = jnp.sum(normal[:, :, None] * unit_dir, axis=0)
    burgers_normal = jnp.sum(burgers * normal, axis=0)[:, None]
    strength = radius_sq / (8.0 * (1.0 - POISSON) * distance_sq)
    field = (1.0 - 2.0 * POISSON) * (
        burgers[:, :, None] * along_n[None] + normal[:, :, None] * along_b[None]
    )
    field = field - burgers_normal[None] * unit_dir + 3.0 * unit_dir * (along_b * along_n)[None]
    return jnp.sum(strength[None] * field, axis=1)


def waves(first, count, total, centre):
    steps = first + jnp.arange(count, dtype=jnp.float32)
    return TWO_PI / LATTICE * (centre + (steps - total * 0.5 + 0.5) / QX)


def factor_block(xcosines, xsines, zcosines, zsines, ytable):
    ywidth = ytable.shape[0] // 2
    left_real = (
        zcosines[None, :, :] * xcosines[:, None, :] - zsines[None, :, :] * xsines[:, None, :]
    )
    left_imag = (
        zcosines[None, :, :] * xsines[:, None, :] + zsines[None, :, :] * xcosines[:, None, :]
    )
    left_pair = jnp.stack([left_real, left_imag], axis=2)
    product = jnp.einsum(
        "xzca,da->xzcd",
        left_pair,
        ytable,
        precision=lax.Precision.HIGH,
        preferred_element_type=jnp.float32,
    )
    real_part = product[:, :, 0, :ywidth] - product[:, :, 1, ywidth:]
    imag_part = product[:, :, 0, ywidth:] + product[:, :, 1, :ywidth]
    return jnp.stack([real_part, imag_part], axis=1)


FINE_STEPS = 16


def sincos_rows(waves_row, values):
    coarse = waves_row[::FINE_STEPS]
    fine = waves_row[:FINE_STEPS] - waves_row[0]
    coarse_angle = coarse[:, None] * values[None, :]
    fine_angle = fine[:, None] * values[None, :]
    cc, sc = jnp.cos(coarse_angle), jnp.sin(coarse_angle)
    cf, sf = jnp.cos(fine_angle), jnp.sin(fine_angle)
    cosines = cc[:, None, :] * cf[None, :, :] - sc[:, None, :] * sf[None, :, :]
    sines = sc[:, None, :] * cf[None, :, :] + cc[:, None, :] * sf[None, :, :]
    shape = (waves_row.shape[0], values.shape[0])
    return cosines.reshape(shape), sines.reshape(shape)


def phase_tables(position, xwaves, ywaves, zwaves):
    xcosines, xsines = sincos_rows(xwaves, position[0])
    ycosines, ysines = sincos_rows(ywaves, position[1])
    zangle = zwaves[:, None] * position[2][None, :]
    ytable = jnp.concatenate([ycosines, ysines], axis=0)
    return (xcosines, xsines, jnp.cos(zangle), jnp.sin(zangle), ytable)


FIELD_ROWS = 16


def field_kernel(table, anchor, out):
    ax, ay, az = anchor[0], anchor[1], anchor[2]

    def one_loop(number, running):
        cx, cy, cz = table[0, number], table[1, number], table[2, number]
        bx, by, bz = table[3, number], table[4, number], table[5, number]
        nx, ny, nz = table[6, number], table[7, number], table[8, number]
        radius_sq, scale, burgers_normal = table[9, number], table[10, number], table[11, number]
        dx, dy, dz = ax - cx, ay - cy, az - cz
        distance_sq = dx * dx + dy * dy + dz * dz + radius_sq
        inverse = lax.rsqrt(distance_sq)
        ux, uy, uz = dx * inverse, dy * inverse, dz * inverse
        along_b = bx * ux + by * uy + bz * uz
        along_n = nx * ux + ny * uy + nz * uz
        strength = scale * (inverse * inverse)
        mixed = 3.0 * (along_b * along_n) - burgers_normal
        fx, fy, fz = running
        gx = (1.0 - 2.0 * POISSON) * (bx * along_n + nx * along_b) + ux * mixed
        gy = (1.0 - 2.0 * POISSON) * (by * along_n + ny * along_b) + uy * mixed
        gz = (1.0 - 2.0 * POISSON) * (bz * along_n + nz * along_b) + uz * mixed
        return (fx + strength * gx, fy + strength * gy, fz + strength * gz)

    zero = jnp.zeros(ax.shape, jnp.float32)
    fx, fy, fz = lax.fori_loop(0, table.shape[1], one_loop, (zero, zero, zero), unroll=4)
    out[0] = fx
    out[1] = fy
    out[2] = fz


def partial_field(anchor, centre, burgers, normal, radius):
    atoms = anchor.shape[1]
    loops = centre.shape[1]
    radius_sq = radius * radius
    scale = radius_sq / (8.0 * (1.0 - POISSON))
    burgers_normal = jnp.sum(burgers * normal, axis=0)
    table = jnp.concatenate(
        [centre, burgers, normal, radius_sq[None], scale[None], burgers_normal[None]], axis=0
    )
    rows = atoms // 128
    tiled = anchor.reshape(3, rows, 128)
    spec = pl.BlockSpec((3, FIELD_ROWS, 128), lambda i: (0, i, 0))
    field = pl.pallas_call(
        field_kernel,
        grid=(rows // FIELD_ROWS,),
        in_specs=[pl.BlockSpec(memory_space=pltpu.SMEM), spec],
        out_specs=spec,
        out_shape=jax.ShapeDtypeStruct(tiled.shape, jnp.float32),
        cost_estimate=pl.CostEstimate(
            flops=55 * atoms * loops, transcendentals=atoms * loops, bytes_accessed=24 * atoms
        ),
    )(table, tiled)
    return field.reshape(3, atoms)


def body(atom_site, loop_cells, loop_burgers, loop_habit, loop_radius):
    anchor = site_anchor(atom_site)
    centre = loop_centre(loop_cells)
    burgers = lookup(loop_burgers, BURGERS_TABLE)
    normal = lookup(loop_habit, NORMAL_TABLE)
    partial_field_value = partial_field(anchor, centre, burgers, normal, loop_radius)
    loop_groups = lax.axis_size("loops")
    chunk = partial_field_value.shape[1] // loop_groups
    owned = lax.all_to_all(
        partial_field_value.reshape(3, loop_groups, chunk), "loops", 1, 1, tiled=True
    ).sum(axis=1)
    displacement = lax.all_to_all(
        jnp.broadcast_to(owned[:, None], (3, loop_groups, chunk)), "loops", 1, 1, tiled=True
    ).reshape(3, -1)
    position = anchor + displacement
    group_count = lax.axis_size("atoms")
    zrows = QZ // lax.axis_size("loops")
    atom_total = position.shape[1] * group_count
    zfirst = (lax.axis_index("loops") * zrows).astype(jnp.float32)
    zwaves = waves(zfirst, zrows, QZ, 0.0)
    ywaves = waves(jnp.float32(0.0), QY, QY, 1.0)
    xwaves = waves(jnp.float32(0.0), QX, QX, 1.0)
    xcosines, xsines, zcosines, zsines, ytable = phase_tables(position, xwaves, ywaves, zwaves)
    partial = factor_block(xcosines, xsines, zcosines, zsines, ytable)
    blocks = partial.reshape(group_count, -1, *partial.shape[1:])
    summed = lax.all_to_all(blocks, "atoms", 0, 0, tiled=True).sum(axis=0)
    power = summed[:, 0] ** 2 + summed[:, 1] ** 2
    return jnp.log1p(jnp.transpose(power, (1, 0, 2)) / atom_total)


def solution(mesh):
    placed = (P("atoms"), P(None, "loops"), P("loops"), P("loops"), P("loops"))
    return jax.shard_map(
        body, mesh=mesh, in_specs=placed, out_specs=P("loops", "atoms", None), check_vma=False
    )
```

```python
import math

import jax
import jax.numpy as jnp
import numpy as np
from jax import lax
from jax.experimental import pallas as pl
from jax.experimental.pallas import tpu as pltpu
from jax.sharding import PartitionSpec as P

WIN_X = 32
WIN_Y = 32
QX = 128
QY = 128
QZ = 64


LATTICE = 2.8665
POISSON = 0.29
TWO_PI = 2.0 * math.pi
BURGERS_TABLE = np.array(
    [[1.0, 1.0, 1.0], [-1.0, 1.0, 1.0], [1.0, -1.0, 1.0], [1.0, 1.0, -1.0]]
) * (0.5 * LATTICE)
NORMAL_TABLE = (
    np.array(
        [
            [1.0, 1.0, 0.0],
            [1.0, -1.0, 0.0],
            [1.0, 0.0, 1.0],
            [1.0, 0.0, -1.0],
            [0.0, 1.0, 1.0],
            [0.0, 1.0, -1.0],
        ]
    )
    * 0.70710678
)


def lookup(index, table):
    columns = []
    for column in range(3):
        total = jnp.zeros(index.shape, jnp.float32)
        for entry in range(table.shape[0]):
            total = total + jnp.where(
                index == entry, jnp.float32(table[entry, column]), jnp.float32(0.0)
            )
        columns.append(total)
    return jnp.stack(columns)


def site_anchor(site):
    basis = site % 2
    cell = site // 2
    first = cell % WIN_X
    second = cell // WIN_X % WIN_Y
    third = cell // (WIN_X * WIN_Y)
    cells = jnp.stack([first, second, third]).astype(jnp.float32)
    return LATTICE * (cells + 0.5 * basis.astype(jnp.float32)[None, :])


def loop_centre(cells):
    return LATTICE * (cells.astype(jnp.float32) + 0.25)


def loop_field(anchor, centre, burgers, normal, radius):
    offset = anchor[:, None, :] - centre[:, :, None]
    radius_sq = (radius * radius)[:, None]
    distance_sq = jnp.sum(offset * offset, axis=0) + radius_sq
    unit_dir = offset * lax.rsqrt(distance_sq)[None]
    along_b = jnp.sum(burgers[:, :, None] * unit_dir, axis=0)
    along_n = jnp.sum(normal[:, :, None] * unit_dir, axis=0)
    burgers_normal = jnp.sum(burgers * normal, axis=0)[:, None]
    strength = radius_sq / (8.0 * (1.0 - POISSON) * distance_sq)
    field = (1.0 - 2.0 * POISSON) * (
        burgers[:, :, None] * along_n[None] + normal[:, :, None] * along_b[None]
    )
    field = field - burgers_normal[None] * unit_dir + 3.0 * unit_dir * (along_b * along_n)[None]
    return jnp.sum(strength[None] * field, axis=1)


def waves(first, count, total, centre):
    steps = first + jnp.arange(count, dtype=jnp.float32)
    return TWO_PI / LATTICE * (centre + (steps - total * 0.5 + 0.5) / QX)


def factor_block(xcosines, xsines, zcosines, zsines, ytable):
    ywidth = ytable.shape[0] // 2
    left_real = (
        zcosines[None, :, :] * xcosines[:, None, :] - zsines[None, :, :] * xsines[:, None, :]
    )
    left_imag = (
        zcosines[None, :, :] * xsines[:, None, :] + zsines[None, :, :] * xcosines[:, None, :]
    )
    left_pair = jnp.stack([left_real, left_imag], axis=2)
    product = jnp.einsum(
        "xzca,da->xzcd",
        left_pair,
        ytable,
        precision=lax.Precision.HIGH,
        preferred_element_type=jnp.float32,
    )
    real_part = product[:, :, 0, :ywidth] - product[:, :, 1, ywidth:]
    imag_part = product[:, :, 0, ywidth:] + product[:, :, 1, :ywidth]
    return jnp.stack([real_part, imag_part], axis=1)


FINE_STEPS = 16


def sincos_rows(waves_row, values):
    coarse = waves_row[::FINE_STEPS]
    fine = waves_row[:FINE_STEPS] - waves_row[0]
    coarse_angle = coarse[:, None] * values[None, :]
    fine_angle = fine[:, None] * values[None, :]
    cc, sc = jnp.cos(coarse_angle), jnp.sin(coarse_angle)
    cf, sf = jnp.cos(fine_angle), jnp.sin(fine_angle)
    cosines = cc[:, None, :] * cf[None, :, :] - sc[:, None, :] * sf[None, :, :]
    sines = sc[:, None, :] * cf[None, :, :] + cc[:, None, :] * sf[None, :, :]
    shape = (waves_row.shape[0], values.shape[0])
    return cosines.reshape(shape), sines.reshape(shape)


def phase_tables(position, xwaves, ywaves, zwaves):
    xcosines, xsines = sincos_rows(xwaves, position[0])
    ycosines, ysines = sincos_rows(ywaves, position[1])
    zangle = zwaves[:, None] * position[2][None, :]
    ytable = jnp.concatenate([ycosines, ysines], axis=0)
    return (xcosines, xsines, jnp.cos(zangle), jnp.sin(zangle), ytable)


HALF_BURGERS = float(BURGERS_TABLE[0, 0])
HABIT_SCALE = float(NORMAL_TABLE[0, 0])
STRENGTH_SCALE = 1.0 / (8.0 * (1.0 - POISSON))
FIELD_SPLIT = 2


def field_kernel(cells, burgers_index, habit_index, radius, site, anchor_out, field_out):
    whole = site[...]
    basis = jnp.bitwise_and(whole, 1)
    cell = jnp.right_shift(whole, 1)
    first = jnp.bitwise_and(cell, WIN_X - 1)
    second = jnp.bitwise_and(jnp.right_shift(cell, 5), WIN_Y - 1)
    third = jnp.right_shift(cell, 10)
    half = 0.5 * basis.astype(jnp.float32)
    coords = [LATTICE * (c.astype(jnp.float32) + half) for c in (first, second, third)]
    for axis in range(3):
        anchor_out[axis] = coords[axis]
    rows = whole.shape[0] // FIELD_SPLIT
    pieces = [[c[p * rows : (p + 1) * rows] for c in coords] for p in range(FIELD_SPLIT)]

    def one_loop(number, running):
        cx = LATTICE * (cells[0, number].astype(jnp.float32) + 0.25)
        cy = LATTICE * (cells[1, number].astype(jnp.float32) + 0.25)
        cz = LATTICE * (cells[2, number].astype(jnp.float32) + 0.25)
        kb = burgers_index[number]
        kh = habit_index[number]
        h = jnp.float32(HALF_BURGERS)
        bx = jnp.where(kb == 1, -h, h)
        by = jnp.where(kb == 2, -h, h)
        bz = jnp.where(kb == 3, -h, h)
        c = jnp.float32(HABIT_SCALE)
        zero = jnp.float32(0.0)
        nx = jnp.where(kh < 4, c, zero)
        ny = jnp.where(kh == 1, -c, jnp.where((kh == 2) | (kh == 3), zero, c))
        nz = jnp.where((kh == 2) | (kh == 4), c, jnp.where((kh == 3) | (kh == 5), -c, zero))
        burgers_normal = bx * nx + by * ny + bz * nz
        r = radius[number]
        radius_sq = r * r
        scale = radius_sq * jnp.float32(STRENGTH_SCALE)
        out = []
        for p in range(FIELD_SPLIT):
            ax, ay, az = pieces[p]
            fx, fy, fz = running[p]
            dx, dy, dz = ax - cx, ay - cy, az - cz
            distance_sq = dx * dx + dy * dy + dz * dz + radius_sq
            inverse = lax.rsqrt(distance_sq)
            ux, uy, uz = dx * inverse, dy * inverse, dz * inverse
            along_b = bx * ux + by * uy + bz * uz
            along_n = nx * ux + ny * uy + nz * uz
            strength = scale * (inverse * inverse)
            mixed = 3.0 * (along_b * along_n) - burgers_normal
            gx = (1.0 - 2.0 * POISSON) * (bx * along_n + nx * along_b) + ux * mixed
            gy = (1.0 - 2.0 * POISSON) * (by * along_n + ny * along_b) + uy * mixed
            gz = (1.0 - 2.0 * POISSON) * (bz * along_n + nz * along_b) + uz * mixed
            out.append((fx + strength * gx, fy + strength * gy, fz + strength * gz))
        return tuple(out)

    zero = jnp.zeros((rows, whole.shape[1]), jnp.float32)
    start = tuple((zero, zero, zero) for _ in range(FIELD_SPLIT))
    totals = lax.fori_loop(0, radius.shape[0], one_loop, start, unroll=2)
    for p in range(FIELD_SPLIT):
        for axis in range(3):
            field_out[axis, p * rows : (p + 1) * rows] = totals[p][axis]


def anchor_and_field(atom_site, loop_cells, loop_burgers, loop_habit, loop_radius):
    atoms = atom_site.shape[0]
    loops = loop_radius.shape[0]
    tiled = atom_site.reshape(atoms // 128, 128)
    smem = pl.BlockSpec(memory_space=pltpu.SMEM)
    vmem = pl.BlockSpec(memory_space=pltpu.VMEM)
    shape = jax.ShapeDtypeStruct((3, *tiled.shape), jnp.float32)
    anchor, field = pl.pallas_call(
        field_kernel,
        in_specs=[smem, smem, smem, smem, vmem],
        out_specs=[vmem, vmem],
        out_shape=[shape, shape],
        cost_estimate=pl.CostEstimate(
            flops=55 * atoms * loops, transcendentals=atoms * loops, bytes_accessed=28 * atoms
        ),
    )(loop_cells, loop_burgers, loop_habit, loop_radius, tiled)
    return anchor.reshape(3, atoms), field

def body(atom_site, loop_cells, loop_burgers, loop_habit, loop_radius):
    anchor, field = anchor_and_field(atom_site, loop_cells, loop_burgers, loop_habit, loop_radius)
    loop_groups = lax.axis_size("loops")
    rows = field.shape[1] // loop_groups
    owned = lax.all_to_all(
        field.reshape(3, loop_groups, rows, field.shape[2]), "loops", 1, 1, tiled=True
    ).sum(axis=1)
    displacement = lax.all_to_all(
        jnp.broadcast_to(owned[:, None], (3, loop_groups, *owned.shape[1:])), "loops", 1, 1, tiled=True
    ).reshape(3, -1)
    position = anchor + displacement
    group_count = lax.axis_size("atoms")
    zrows = QZ // lax.axis_size("loops")
    atom_total = position.shape[1] * group_count
    zfirst = (lax.axis_index("loops") * zrows).astype(jnp.float32)
    zwaves = waves(zfirst, zrows, QZ, 0.0)
    ywaves = waves(jnp.float32(0.0), QY, QY, 1.0)
    xwaves = waves(jnp.float32(0.0), QX, QX, 1.0)
    xcosines, xsines, zcosines, zsines, ytable = phase_tables(position, xwaves, ywaves, zwaves)
    partial = factor_block(xcosines, xsines, zcosines, zsines, ytable)
    blocks = partial.reshape(group_count, -1, *partial.shape[1:])
    summed = lax.all_to_all(blocks, "atoms", 0, 0, tiled=True).sum(axis=0)
    power = summed[:, 0] ** 2 + summed[:, 1] ** 2
    return jnp.log1p(jnp.transpose(power, (1, 0, 2)) / atom_total)


def solution(mesh):
    placed = (P("atoms"), P(None, "loops"), P("loops"), P("loops"), P("loops"))
    return jax.shard_map(
        body, mesh=mesh, in_specs=placed, out_specs=P("loops", "atoms", None), check_vma=False
    )
```

```python
import math

import jax
import jax.numpy as jnp
import numpy as np
from jax import lax
from jax.experimental import pallas as pl
from jax.experimental.pallas import tpu as pltpu
from jax.sharding import Mesh, PartitionSpec as P

WIN_X = 32
WIN_Y = 32
QX = 128
QY = 128
QZ = 64


LATTICE = 2.8665
POISSON = 0.29
TWO_PI = 2.0 * math.pi
BURGERS_TABLE = np.array(
    [[1.0, 1.0, 1.0], [-1.0, 1.0, 1.0], [1.0, -1.0, 1.0], [1.0, 1.0, -1.0]]
) * (0.5 * LATTICE)
NORMAL_TABLE = (
    np.array(
        [
            [1.0, 1.0, 0.0],
            [1.0, -1.0, 0.0],
            [1.0, 0.0, 1.0],
            [1.0, 0.0, -1.0],
            [0.0, 1.0, 1.0],
            [0.0, 1.0, -1.0],
        ]
    )
    * 0.70710678
)


def lookup(index, table):
    columns = []
    for column in range(3):
        total = jnp.zeros(index.shape, jnp.float32)
        for entry in range(table.shape[0]):
            total = total + jnp.where(
                index == entry, jnp.float32(table[entry, column]), jnp.float32(0.0)
            )
        columns.append(total)
    return jnp.stack(columns)


def site_anchor(site):
    basis = site % 2
    cell = site // 2
    first = cell % WIN_X
    second = cell // WIN_X % WIN_Y
    third = cell // (WIN_X * WIN_Y)
    cells = jnp.stack([first, second, third]).astype(jnp.float32)
    return LATTICE * (cells + 0.5 * basis.astype(jnp.float32)[None, :])


def loop_centre(cells):
    return LATTICE * (cells.astype(jnp.float32) + 0.25)


def loop_field(anchor, centre, burgers, normal, radius):
    offset = anchor[:, None, :] - centre[:, :, None]
    radius_sq = (radius * radius)[:, None]
    distance_sq = jnp.sum(offset * offset, axis=0) + radius_sq
    unit_dir = offset * lax.rsqrt(distance_sq)[None]
    along_b = jnp.sum(burgers[:, :, None] * unit_dir, axis=0)
    along_n = jnp.sum(normal[:, :, None] * unit_dir, axis=0)
    burgers_normal = jnp.sum(burgers * normal, axis=0)[:, None]
    strength = radius_sq / (8.0 * (1.0 - POISSON) * distance_sq)
    field = (1.0 - 2.0 * POISSON) * (
        burgers[:, :, None] * along_n[None] + normal[:, :, None] * along_b[None]
    )
    field = field - burgers_normal[None] * unit_dir + 3.0 * unit_dir * (along_b * along_n)[None]
    return jnp.sum(strength[None] * field, axis=1)


def waves(first, count, total, centre):
    steps = first + jnp.arange(count, dtype=jnp.float32)
    return TWO_PI / LATTICE * (centre + (steps - total * 0.5 + 0.5) / QX)


def factor_block(xcosines, xsines, zcosines, zsines, ytable):
    ywidth = ytable.shape[0] // 2
    left_real = (
        zcosines[None, :, :] * xcosines[:, None, :] - zsines[None, :, :] * xsines[:, None, :]
    )
    left_imag = (
        zcosines[None, :, :] * xsines[:, None, :] + zsines[None, :, :] * xcosines[:, None, :]
    )
    left_pair = jnp.stack([left_real, left_imag], axis=2)
    product = jnp.einsum(
        "xzca,da->xzcd",
        left_pair,
        ytable,
        precision=lax.Precision.HIGH,
        preferred_element_type=jnp.float32,
    )
    real_part = product[:, :, 0, :ywidth] - product[:, :, 1, ywidth:]
    imag_part = product[:, :, 0, ywidth:] + product[:, :, 1, :ywidth]
    return jnp.stack([real_part, imag_part], axis=1)


FINE_STEPS = 16


def sincos_rows(waves_row, values):
    coarse = waves_row[::FINE_STEPS]
    fine = waves_row[:FINE_STEPS] - waves_row[0]
    coarse_angle = coarse[:, None] * values[None, :]
    fine_angle = fine[:, None] * values[None, :]
    cc, sc = jnp.cos(coarse_angle), jnp.sin(coarse_angle)
    cf, sf = jnp.cos(fine_angle), jnp.sin(fine_angle)
    cosines = cc[:, None, :] * cf[None, :, :] - sc[:, None, :] * sf[None, :, :]
    sines = sc[:, None, :] * cf[None, :, :] + cc[:, None, :] * sf[None, :, :]
    shape = (waves_row.shape[0], values.shape[0])
    return cosines.reshape(shape), sines.reshape(shape)


def phase_tables(position, xwaves, ywaves, zwaves):
    xcosines, xsines = sincos_rows(xwaves, position[0])
    ycosines, ysines = sincos_rows(ywaves, position[1])
    zangle = zwaves[:, None] * position[2][None, :]
    ytable = jnp.concatenate([ycosines, ysines], axis=0)
    return (xcosines, xsines, jnp.cos(zangle), jnp.sin(zangle), ytable)


HALF_BURGERS = float(BURGERS_TABLE[0, 0])
HABIT_SCALE = float(NORMAL_TABLE[0, 0])
STRENGTH_SCALE = 1.0 / (8.0 * (1.0 - POISSON))
FIELD_SPLIT = 2


def field_kernel(cells, burgers_index, habit_index, radius, site, anchor_out, field_out):
    whole = site[...]
    basis = jnp.bitwise_and(whole, 1)
    cell = jnp.right_shift(whole, 1)
    first = jnp.bitwise_and(cell, WIN_X - 1)
    second = jnp.bitwise_and(jnp.right_shift(cell, 5), WIN_Y - 1)
    third = jnp.right_shift(cell, 10)
    half = 0.5 * basis.astype(jnp.float32)
    coords = [LATTICE * (c.astype(jnp.float32) + half) for c in (first, second, third)]
    for axis in range(3):
        anchor_out[axis] = coords[axis]
    rows = whole.shape[0] // FIELD_SPLIT
    pieces = [[c[p * rows : (p + 1) * rows] for c in coords] for p in range(FIELD_SPLIT)]

    def one_loop(number, running):
        cx = LATTICE * (cells[0, number].astype(jnp.float32) + 0.25)
        cy = LATTICE * (cells[1, number].astype(jnp.float32) + 0.25)
        cz = LATTICE * (cells[2, number].astype(jnp.float32) + 0.25)
        kb = burgers_index[number]
        kh = habit_index[number]
        h = jnp.float32(HALF_BURGERS)
        bx = jnp.where(kb == 1, -h, h)
        by = jnp.where(kb == 2, -h, h)
        bz = jnp.where(kb == 3, -h, h)
        c = jnp.float32(HABIT_SCALE)
        zero = jnp.float32(0.0)
        nx = jnp.where(kh < 4, c, zero)
        ny = jnp.where(kh == 1, -c, jnp.where((kh == 2) | (kh == 3), zero, c))
        nz = jnp.where((kh == 2) | (kh == 4), c, jnp.where((kh == 3) | (kh == 5), -c, zero))
        burgers_normal = bx * nx + by * ny + bz * nz
        r = radius[number]
        radius_sq = r * r
        scale = radius_sq * jnp.float32(STRENGTH_SCALE)
        out = []
        for p in range(FIELD_SPLIT):
            ax, ay, az = pieces[p]
            fx, fy, fz = running[p]
            dx, dy, dz = ax - cx, ay - cy, az - cz
            distance_sq = dx * dx + dy * dy + dz * dz + radius_sq
            inverse = lax.rsqrt(distance_sq)
            ux, uy, uz = dx * inverse, dy * inverse, dz * inverse
            along_b = bx * ux + by * uy + bz * uz
            along_n = nx * ux + ny * uy + nz * uz
            strength = scale * (inverse * inverse)
            mixed = 3.0 * (along_b * along_n) - burgers_normal
            gx = (1.0 - 2.0 * POISSON) * (bx * along_n + nx * along_b) + ux * mixed
            gy = (1.0 - 2.0 * POISSON) * (by * along_n + ny * along_b) + uy * mixed
            gz = (1.0 - 2.0 * POISSON) * (bz * along_n + nz * along_b) + uz * mixed
            out.append((fx + strength * gx, fy + strength * gy, fz + strength * gz))
        return tuple(out)

    zero = jnp.zeros((rows, whole.shape[1]), jnp.float32)
    start = tuple((zero, zero, zero) for _ in range(FIELD_SPLIT))
    totals = lax.fori_loop(0, radius.shape[0], one_loop, start, unroll=2)
    for p in range(FIELD_SPLIT):
        for axis in range(3):
            field_out[axis, p * rows : (p + 1) * rows] = totals[p][axis]


def anchor_and_field(atom_site, loop_cells, loop_burgers, loop_habit, loop_radius):
    atoms = atom_site.shape[0]
    loops = loop_radius.shape[0]
    tiled = atom_site.reshape(atoms // 128, 128)
    smem = pl.BlockSpec(memory_space=pltpu.SMEM)
    vmem = pl.BlockSpec(memory_space=pltpu.VMEM)
    shape = jax.ShapeDtypeStruct((3, *tiled.shape), jnp.float32)
    anchor, field = pl.pallas_call(
        field_kernel,
        in_specs=[smem, smem, smem, smem, vmem],
        out_specs=[vmem, vmem],
        out_shape=[shape, shape],
        cost_estimate=pl.CostEstimate(
            flops=55 * atoms * loops, transcendentals=atoms * loops, bytes_accessed=28 * atoms
        ),
    )(loop_cells, loop_burgers, loop_habit, loop_radius, tiled)
    return anchor.reshape(3, atoms), field

def body(atom_site, loop_cells, loop_burgers, loop_habit, loop_radius):
    anchor, field = anchor_and_field(atom_site, loop_cells, loop_burgers, loop_habit, loop_radius)
    loop_groups = lax.axis_size("loops")
    rows = field.shape[1] // loop_groups
    owned = lax.all_to_all(
        field.reshape(3, loop_groups, rows, field.shape[2]), "loops", 1, 1, tiled=True
    ).sum(axis=1)
    displacement = lax.all_to_all(
        jnp.broadcast_to(owned[:, None], (3, loop_groups, *owned.shape[1:])), "loops", 1, 1, tiled=True
    ).reshape(3, -1)
    position = anchor + displacement
    group_count = lax.axis_size((ATOM_OUTER, ATOM_CORE))
    zrows = QZ // lax.axis_size("loops")
    atom_total = position.shape[1] * group_count
    zfirst = (lax.axis_index("loops") * zrows).astype(jnp.float32)
    zwaves = waves(zfirst, zrows, QZ, 0.0)
    ywaves = waves(jnp.float32(0.0), QY, QY, 1.0)
    xwaves = waves(jnp.float32(0.0), QX, QX, 1.0)
    xcosines, xsines, zcosines, zsines, ytable = phase_tables(position, xwaves, ywaves, zwaves)
    outer = lax.axis_size(ATOM_OUTER)
    core = lax.axis_index(ATOM_CORE)
    split = (outer, 2, xcosines.shape[0] // (2 * outer), xcosines.shape[1])

    def rows_of(table, side):
        picked = lax.dynamic_index_in_dim(table.reshape(split), side, axis=1, keepdims=False)
        return picked.reshape(-1, table.shape[1])

    away = 1 - core
    sent = factor_block(rows_of(xcosines, away), rows_of(xsines, away), zcosines, zsines, ytable)
    arrived = lax.ppermute(sent, ATOM_CORE, [(0, 1), (1, 0)])
    kept = factor_block(rows_of(xcosines, core), rows_of(xsines, core), zcosines, zsines, ytable)
    partial = kept + arrived
    blocks = partial.reshape(outer, -1, *partial.shape[1:])
    summed = lax.all_to_all(blocks, ATOM_OUTER, 0, 0, tiled=True).sum(axis=0)
    power = summed[:, 0] ** 2 + summed[:, 1] ** 2
    return jnp.log1p(jnp.transpose(power, (1, 0, 2)) / atom_total)


ATOM_OUTER = "atom_pairs"
ATOM_CORE = "atom_core"


def solution(mesh):
    groups, loop_groups = mesh.devices.shape
    paired = Mesh(
        mesh.devices.reshape(groups // 2, 2, loop_groups), (ATOM_OUTER, ATOM_CORE, "loops")
    )
    atoms = (ATOM_OUTER, ATOM_CORE)
    placed = (P(atoms), P(None, "loops"), P("loops"), P("loops"), P("loops"))
    return jax.shard_map(
        body, mesh=paired, in_specs=placed, out_specs=P("loops", atoms, None), check_vma=False
    )
```

```python
import math

import jax
import jax.numpy as jnp
import numpy as np
from jax import lax
from jax.experimental import pallas as pl
from jax.experimental.pallas import tpu as pltpu
from jax.sharding import Mesh, PartitionSpec as P

WIN_X = 32
WIN_Y = 32
QX = 128
QY = 128
QZ = 64


LATTICE = 2.8665
POISSON = 0.29
TWO_PI = 2.0 * math.pi
BURGERS_TABLE = np.array(
    [[1.0, 1.0, 1.0], [-1.0, 1.0, 1.0], [1.0, -1.0, 1.0], [1.0, 1.0, -1.0]]
) * (0.5 * LATTICE)
NORMAL_TABLE = (
    np.array(
        [
            [1.0, 1.0, 0.0],
            [1.0, -1.0, 0.0],
            [1.0, 0.0, 1.0],
            [1.0, 0.0, -1.0],
            [0.0, 1.0, 1.0],
            [0.0, 1.0, -1.0],
        ]
    )
    * 0.70710678
)


def lookup(index, table):
    columns = []
    for column in range(3):
        total = jnp.zeros(index.shape, jnp.float32)
        for entry in range(table.shape[0]):
            total = total + jnp.where(
                index == entry, jnp.float32(table[entry, column]), jnp.float32(0.0)
            )
        columns.append(total)
    return jnp.stack(columns)


def site_anchor(site):
    basis = site % 2
    cell = site // 2
    first = cell % WIN_X
    second = cell // WIN_X % WIN_Y
    third = cell // (WIN_X * WIN_Y)
    cells = jnp.stack([first, second, third]).astype(jnp.float32)
    return LATTICE * (cells + 0.5 * basis.astype(jnp.float32)[None, :])


def loop_centre(cells):
    return LATTICE * (cells.astype(jnp.float32) + 0.25)


def loop_field(anchor, centre, burgers, normal, radius):
    offset = anchor[:, None, :] - centre[:, :, None]
    radius_sq = (radius * radius)[:, None]
    distance_sq = jnp.sum(offset * offset, axis=0) + radius_sq
    unit_dir = offset * lax.rsqrt(distance_sq)[None]
    along_b = jnp.sum(burgers[:, :, None] * unit_dir, axis=0)
    along_n = jnp.sum(normal[:, :, None] * unit_dir, axis=0)
    burgers_normal = jnp.sum(burgers * normal, axis=0)[:, None]
    strength = radius_sq / (8.0 * (1.0 - POISSON) * distance_sq)
    field = (1.0 - 2.0 * POISSON) * (
        burgers[:, :, None] * along_n[None] + normal[:, :, None] * along_b[None]
    )
    field = field - burgers_normal[None] * unit_dir + 3.0 * unit_dir * (along_b * along_n)[None]
    return jnp.sum(strength[None] * field, axis=1)


def waves(first, count, total, centre):
    steps = first + jnp.arange(count, dtype=jnp.float32)
    return TWO_PI / LATTICE * (centre + (steps - total * 0.5 + 0.5) / QX)


def factor_block(xcosines, xsines, zcosines, zsines, ytable):
    ywidth = ytable.shape[0] // 2
    left_real = (
        zcosines[None, :, :] * xcosines[:, None, :] - zsines[None, :, :] * xsines[:, None, :]
    )
    left_imag = (
        zcosines[None, :, :] * xsines[:, None, :] + zsines[None, :, :] * xcosines[:, None, :]
    )
    left_pair = jnp.stack([left_real, left_imag], axis=2)
    product = jnp.einsum(
        "xzca,da->xzcd",
        left_pair,
        ytable,
        precision=lax.Precision.HIGH,
        preferred_element_type=jnp.float32,
    )
    real_part = product[:, :, 0, :ywidth] - product[:, :, 1, ywidth:]
    imag_part = product[:, :, 0, ywidth:] + product[:, :, 1, :ywidth]
    return jnp.stack([real_part, imag_part], axis=1)


FINE_STEPS = 16


def sincos_rows(coarse, fine, values):
    coarse_angle = coarse[:, None] * values[None, :]
    fine_angle = fine[:, None] * values[None, :]
    cc, sc = jnp.cos(coarse_angle), jnp.sin(coarse_angle)
    cf, sf = jnp.cos(fine_angle), jnp.sin(fine_angle)
    cosines = cc[:, None, :] * cf[None, :, :] - sc[:, None, :] * sf[None, :, :]
    sines = sc[:, None, :] * cf[None, :, :] + cc[:, None, :] * sf[None, :, :]
    shape = (coarse.shape[0] * fine.shape[0], values.shape[0])
    return cosines.reshape(shape), sines.reshape(shape)


def steps_of(waves_row, picked=None):
    fine = waves_row[:FINE_STEPS] - waves_row[0]
    if picked is not None:
        fine = jnp.take(fine, picked)
    return waves_row[::FINE_STEPS], fine


def phase_tables(position, ywaves, zwaves):
    ycosines, ysines = sincos_rows(*steps_of(ywaves), position[1])
    zangle = zwaves[:, None] * position[2][None, :]
    ytable = jnp.concatenate([ycosines, ysines], axis=0)
    return jnp.cos(zangle), jnp.sin(zangle), ytable


HALF_BURGERS = float(BURGERS_TABLE[0, 0])
HABIT_SCALE = float(NORMAL_TABLE[0, 0])
STRENGTH_SCALE = 1.0 / (8.0 * (1.0 - POISSON))
FIELD_SPLIT = 2


def field_kernel(cells, burgers_index, habit_index, radius, site, anchor_out, field_out):
    whole = site[...]
    basis = jnp.bitwise_and(whole, 1)
    cell = jnp.right_shift(whole, 1)
    first = jnp.bitwise_and(cell, WIN_X - 1)
    second = jnp.bitwise_and(jnp.right_shift(cell, 5), WIN_Y - 1)
    third = jnp.right_shift(cell, 10)
    half = 0.5 * basis.astype(jnp.float32)
    coords = [LATTICE * (c.astype(jnp.float32) + half) for c in (first, second, third)]
    for axis in range(3):
        anchor_out[axis] = coords[axis]
    rows = whole.shape[0] // FIELD_SPLIT
    pieces = [[c[p * rows : (p + 1) * rows] for c in coords] for p in range(FIELD_SPLIT)]

    def one_loop(number, running):
        cx = LATTICE * (cells[0, number].astype(jnp.float32) + 0.25)
        cy = LATTICE * (cells[1, number].astype(jnp.float32) + 0.25)
        cz = LATTICE * (cells[2, number].astype(jnp.float32) + 0.25)
        kb = burgers_index[number]
        kh = habit_index[number]
        h = jnp.float32(HALF_BURGERS)
        bx = jnp.where(kb == 1, -h, h)
        by = jnp.where(kb == 2, -h, h)
        bz = jnp.where(kb == 3, -h, h)
        c = jnp.float32(HABIT_SCALE)
        zero = jnp.float32(0.0)
        nx = jnp.where(kh < 4, c, zero)
        ny = jnp.where(kh == 1, -c, jnp.where((kh == 2) | (kh == 3), zero, c))
        nz = jnp.where((kh == 2) | (kh == 4), c, jnp.where((kh == 3) | (kh == 5), -c, zero))
        burgers_normal = bx * nx + by * ny + bz * nz
        r = radius[number]
        radius_sq = r * r
        scale = radius_sq * jnp.float32(STRENGTH_SCALE)
        out = []
        for p in range(FIELD_SPLIT):
            ax, ay, az = pieces[p]
            fx, fy, fz = running[p]
            dx, dy, dz = ax - cx, ay - cy, az - cz
            distance_sq = dx * dx + dy * dy + dz * dz + radius_sq
            inverse = lax.rsqrt(distance_sq)
            ux, uy, uz = dx * inverse, dy * inverse, dz * inverse
            along_b = bx * ux + by * uy + bz * uz
            along_n = nx * ux + ny * uy + nz * uz
            strength = scale * (inverse * inverse)
            mixed = 3.0 * (along_b * along_n) - burgers_normal
            gx = (1.0 - 2.0 * POISSON) * (bx * along_n + nx * along_b) + ux * mixed
            gy = (1.0 - 2.0 * POISSON) * (by * along_n + ny * along_b) + uy * mixed
            gz = (1.0 - 2.0 * POISSON) * (bz * along_n + nz * along_b) + uz * mixed
            out.append((fx + strength * gx, fy + strength * gy, fz + strength * gz))
        return tuple(out)

    zero = jnp.zeros((rows, whole.shape[1]), jnp.float32)
    start = tuple((zero, zero, zero) for _ in range(FIELD_SPLIT))
    totals = lax.fori_loop(0, radius.shape[0], one_loop, start, unroll=2)
    for p in range(FIELD_SPLIT):
        for axis in range(3):
            field_out[axis, p * rows : (p + 1) * rows] = totals[p][axis]


def anchor_and_field(atom_site, loop_cells, loop_burgers, loop_habit, loop_radius):
    atoms = atom_site.shape[0]
    loops = loop_radius.shape[0]
    tiled = atom_site.reshape(atoms // 128, 128)
    smem = pl.BlockSpec(memory_space=pltpu.SMEM)
    vmem = pl.BlockSpec(memory_space=pltpu.VMEM)
    shape = jax.ShapeDtypeStruct((3, *tiled.shape), jnp.float32)
    anchor, field = pl.pallas_call(
        field_kernel,
        in_specs=[smem, smem, smem, smem, vmem],
        out_specs=[vmem, vmem],
        out_shape=[shape, shape],
        cost_estimate=pl.CostEstimate(
            flops=55 * atoms * loops, transcendentals=atoms * loops, bytes_accessed=28 * atoms
        ),
    )(loop_cells, loop_burgers, loop_habit, loop_radius, tiled)
    return anchor.reshape(3, atoms), field

def body(atom_site, loop_cells, loop_burgers, loop_habit, loop_radius):
    anchor, field = anchor_and_field(atom_site, loop_cells, loop_burgers, loop_habit, loop_radius)
    loop_groups = lax.axis_size("loops")
    rows = field.shape[1] // loop_groups
    owned = lax.all_to_all(
        field.reshape(3, loop_groups, rows, field.shape[2]), "loops", 1, 1, tiled=True
    ).sum(axis=1)
    displacement = lax.all_to_all(
        jnp.broadcast_to(owned[:, None], (3, loop_groups, *owned.shape[1:])), "loops", 1, 1, tiled=True
    ).reshape(3, -1)
    position = anchor + displacement
    group_count = lax.axis_size((ATOM_OUTER, ATOM_CORE))
    zrows = QZ // lax.axis_size("loops")
    atom_total = position.shape[1] * group_count
    zfirst = (lax.axis_index("loops") * zrows).astype(jnp.float32)
    zwaves = waves(zfirst, zrows, QZ, 0.0)
    ywaves = waves(jnp.float32(0.0), QY, QY, 1.0)
    xwaves = waves(jnp.float32(0.0), QX, QX, 1.0)
    zcosines, zsines, ytable = phase_tables(position, ywaves, zwaves)
    outer = lax.axis_size(ATOM_OUTER)
    core = lax.axis_index(ATOM_CORE)
    block = QX // (2 * outer)
    lanes = np.arange(FINE_STEPS)
    first_side = jnp.asarray(lanes[(lanes // block) % 2 == 0], jnp.int32)

    def half(side):
        xcosines, xsines = sincos_rows(*steps_of(xwaves, first_side + block * side), position[0])
        return factor_block(xcosines, xsines, zcosines, zsines, ytable)

    sent = half(1 - core)
    arrived = lax.ppermute(sent, ATOM_CORE, [(0, 1), (1, 0)])
    kept = half(core)
    partial = kept + arrived
    blocks = partial.reshape(outer, -1, *partial.shape[1:])
    summed = lax.all_to_all(blocks, ATOM_OUTER, 0, 0, tiled=True).sum(axis=0)
    power = summed[:, 0] ** 2 + summed[:, 1] ** 2
    return jnp.log1p(jnp.transpose(power, (1, 0, 2)) / atom_total)


ATOM_OUTER = "atom_pairs"
ATOM_CORE = "atom_core"


def solution(mesh):
    groups, loop_groups = mesh.devices.shape
    paired = Mesh(
        mesh.devices.reshape(groups // 2, 2, loop_groups), (ATOM_OUTER, ATOM_CORE, "loops")
    )
    atoms = (ATOM_OUTER, ATOM_CORE)
    placed = (P(atoms), P(None, "loops"), P("loops"), P("loops"), P("loops"))
    return jax.shard_map(
        body, mesh=paired, in_specs=placed, out_specs=P("loops", atoms, None), check_vma=False
    )
```

```python
import math

import jax
import jax.numpy as jnp
import numpy as np
from jax import lax
from jax.experimental import pallas as pl
from jax.experimental.pallas import tpu as pltpu
from jax.sharding import Mesh, PartitionSpec as P

WIN_X = 32
WIN_Y = 32
QX = 128
QY = 128
QZ = 64


LATTICE = 2.8665
POISSON = 0.29
TWO_PI = 2.0 * math.pi
BURGERS_TABLE = np.array(
    [[1.0, 1.0, 1.0], [-1.0, 1.0, 1.0], [1.0, -1.0, 1.0], [1.0, 1.0, -1.0]]
) * (0.5 * LATTICE)
NORMAL_TABLE = (
    np.array(
        [
            [1.0, 1.0, 0.0],
            [1.0, -1.0, 0.0],
            [1.0, 0.0, 1.0],
            [1.0, 0.0, -1.0],
            [0.0, 1.0, 1.0],
            [0.0, 1.0, -1.0],
        ]
    )
    * 0.70710678
)


def lookup(index, table):
    columns = []
    for column in range(3):
        total = jnp.zeros(index.shape, jnp.float32)
        for entry in range(table.shape[0]):
            total = total + jnp.where(
                index == entry, jnp.float32(table[entry, column]), jnp.float32(0.0)
            )
        columns.append(total)
    return jnp.stack(columns)


def site_anchor(site):
    basis = site % 2
    cell = site // 2
    first = cell % WIN_X
    second = cell // WIN_X % WIN_Y
    third = cell // (WIN_X * WIN_Y)
    cells = jnp.stack([first, second, third]).astype(jnp.float32)
    return LATTICE * (cells + 0.5 * basis.astype(jnp.float32)[None, :])


def loop_centre(cells):
    return LATTICE * (cells.astype(jnp.float32) + 0.25)


def loop_field(anchor, centre, burgers, normal, radius):
    offset = anchor[:, None, :] - centre[:, :, None]
    radius_sq = (radius * radius)[:, None]
    distance_sq = jnp.sum(offset * offset, axis=0) + radius_sq
    unit_dir = offset * lax.rsqrt(distance_sq)[None]
    along_b = jnp.sum(burgers[:, :, None] * unit_dir, axis=0)
    along_n = jnp.sum(normal[:, :, None] * unit_dir, axis=0)
    burgers_normal = jnp.sum(burgers * normal, axis=0)[:, None]
    strength = radius_sq / (8.0 * (1.0 - POISSON) * distance_sq)
    field = (1.0 - 2.0 * POISSON) * (
        burgers[:, :, None] * along_n[None] + normal[:, :, None] * along_b[None]
    )
    field = field - burgers_normal[None] * unit_dir + 3.0 * unit_dir * (along_b * along_n)[None]
    return jnp.sum(strength[None] * field, axis=1)


def waves(first, count, total, centre):
    steps = first + jnp.arange(count, dtype=jnp.float32)
    return TWO_PI / LATTICE * (centre + (steps - total * 0.5 + 0.5) / QX)


def factor_block(xcosines, xsines, zcosines, zsines, ytable):
    ywidth = ytable.shape[0] // 2
    left_real = (
        zcosines[None, :, :] * xcosines[:, None, :] - zsines[None, :, :] * xsines[:, None, :]
    )
    left_imag = (
        zcosines[None, :, :] * xsines[:, None, :] + zsines[None, :, :] * xcosines[:, None, :]
    )
    left_pair = jnp.stack([left_real, left_imag], axis=2)
    product = jnp.einsum(
        "xzca,da->xzcd",
        left_pair,
        ytable,
        precision=lax.Precision.HIGH,
        preferred_element_type=jnp.float32,
    )
    real_part = product[:, :, 0, :ywidth] - product[:, :, 1, ywidth:]
    imag_part = product[:, :, 0, ywidth:] + product[:, :, 1, :ywidth]
    return jnp.stack([real_part, imag_part], axis=1)


FINE_STEPS = 16


def sincos_rows(coarse, fine, values, fine_major=False):
    coarse_angle = coarse[:, None] * values[None, :]
    fine_angle = fine[:, None] * values[None, :]
    cc, sc = jnp.cos(coarse_angle), jnp.sin(coarse_angle)
    cf, sf = jnp.cos(fine_angle), jnp.sin(fine_angle)
    if fine_major:
        cc, sc, cf, sf = cf, sf, cc, sc
    cosines = cc[:, None, :] * cf[None, :, :] - sc[:, None, :] * sf[None, :, :]
    sines = sc[:, None, :] * cf[None, :, :] + cc[:, None, :] * sf[None, :, :]
    shape = (coarse.shape[0] * fine.shape[0], values.shape[0])
    return cosines.reshape(shape), sines.reshape(shape)


def steps_of(waves_row, picked=None):
    fine = waves_row[:FINE_STEPS] - waves_row[0]
    if picked is not None:
        fine = jnp.take(fine, picked)
    return waves_row[::FINE_STEPS], fine


def phase_tables(position, ywaves, zwaves):
    ycosines, ysines = sincos_rows(*steps_of(ywaves), position[1])
    zangle = zwaves[:, None] * position[2][None, :]
    ytable = jnp.concatenate([ycosines, ysines], axis=0)
    return jnp.cos(zangle), jnp.sin(zangle), ytable


HALF_BURGERS = float(BURGERS_TABLE[0, 0])
HABIT_SCALE = float(NORMAL_TABLE[0, 0])
STRENGTH_SCALE = 1.0 / (8.0 * (1.0 - POISSON))
FIELD_SPLIT = 2


def field_kernel(cells, burgers_index, habit_index, radius, site, anchor_out, field_out):
    whole = site[...]
    basis = jnp.bitwise_and(whole, 1)
    cell = jnp.right_shift(whole, 1)
    first = jnp.bitwise_and(cell, WIN_X - 1)
    second = jnp.bitwise_and(jnp.right_shift(cell, 5), WIN_Y - 1)
    third = jnp.right_shift(cell, 10)
    half = 0.5 * basis.astype(jnp.float32)
    coords = [LATTICE * (c.astype(jnp.float32) + half) for c in (first, second, third)]
    for axis in range(3):
        anchor_out[axis] = coords[axis]
    rows = whole.shape[0] // FIELD_SPLIT
    pieces = [[c[p * rows : (p + 1) * rows] for c in coords] for p in range(FIELD_SPLIT)]

    def one_loop(number, running):
        cx = LATTICE * (cells[0, number].astype(jnp.float32) + 0.25)
        cy = LATTICE * (cells[1, number].astype(jnp.float32) + 0.25)
        cz = LATTICE * (cells[2, number].astype(jnp.float32) + 0.25)
        kb = burgers_index[number]
        kh = habit_index[number]
        h = jnp.float32(HALF_BURGERS)
        bx = jnp.where(kb == 1, -h, h)
        by = jnp.where(kb == 2, -h, h)
        bz = jnp.where(kb == 3, -h, h)
        c = jnp.float32(HABIT_SCALE)
        zero = jnp.float32(0.0)
        nx = jnp.where(kh < 4, c, zero)
        ny = jnp.where(kh == 1, -c, jnp.where((kh == 2) | (kh == 3), zero, c))
        nz = jnp.where((kh == 2) | (kh == 4), c, jnp.where((kh == 3) | (kh == 5), -c, zero))
        burgers_normal = bx * nx + by * ny + bz * nz
        r = radius[number]
        radius_sq = r * r
        scale = radius_sq * jnp.float32(STRENGTH_SCALE)
        out = []
        for p in range(FIELD_SPLIT):
            ax, ay, az = pieces[p]
            fx, fy, fz = running[p]
            dx, dy, dz = ax - cx, ay - cy, az - cz
            distance_sq = dx * dx + dy * dy + dz * dz + radius_sq
            inverse = lax.rsqrt(distance_sq)
            ux, uy, uz = dx * inverse, dy * inverse, dz * inverse
            along_b = bx * ux + by * uy + bz * uz
            along_n = nx * ux + ny * uy + nz * uz
            strength = scale * (inverse * inverse)
            mixed = 3.0 * (along_b * along_n) - burgers_normal
            gx = (1.0 - 2.0 * POISSON) * (bx * along_n + nx * along_b) + ux * mixed
            gy = (1.0 - 2.0 * POISSON) * (by * along_n + ny * along_b) + uy * mixed
            gz = (1.0 - 2.0 * POISSON) * (bz * along_n + nz * along_b) + uz * mixed
            out.append((fx + strength * gx, fy + strength * gy, fz + strength * gz))
        return tuple(out)

    zero = jnp.zeros((rows, whole.shape[1]), jnp.float32)
    start = tuple((zero, zero, zero) for _ in range(FIELD_SPLIT))
    totals = lax.fori_loop(0, radius.shape[0], one_loop, start, unroll=2)
    for p in range(FIELD_SPLIT):
        for axis in range(3):
            field_out[axis, p * rows : (p + 1) * rows] = totals[p][axis]


def anchor_and_field(atom_site, loop_cells, loop_burgers, loop_habit, loop_radius):
    atoms = atom_site.shape[0]
    loops = loop_radius.shape[0]
    tiled = atom_site.reshape(atoms // 128, 128)
    smem = pl.BlockSpec(memory_space=pltpu.SMEM)
    vmem = pl.BlockSpec(memory_space=pltpu.VMEM)
    shape = jax.ShapeDtypeStruct((3, *tiled.shape), jnp.float32)
    anchor, field = pl.pallas_call(
        field_kernel,
        in_specs=[smem, smem, smem, smem, vmem],
        out_specs=[vmem, vmem],
        out_shape=[shape, shape],
        cost_estimate=pl.CostEstimate(
            flops=55 * atoms * loops, transcendentals=atoms * loops, bytes_accessed=28 * atoms
        ),
    )(loop_cells, loop_burgers, loop_habit, loop_radius, tiled)
    return anchor.reshape(3, atoms), field

def body(atom_site, loop_cells, loop_burgers, loop_habit, loop_radius):
    anchor, field = anchor_and_field(atom_site, loop_cells, loop_burgers, loop_habit, loop_radius)
    loop_groups = lax.axis_size("loops")
    rows = field.shape[1] // loop_groups
    owned = lax.all_to_all(
        field.reshape(3, loop_groups, rows, field.shape[2]), "loops", 1, 1, tiled=True
    ).sum(axis=1)
    displacement = lax.all_to_all(
        jnp.broadcast_to(owned[:, None], (3, loop_groups, *owned.shape[1:])), "loops", 1, 1, tiled=True
    ).reshape(3, -1)
    position = anchor + displacement
    group_count = lax.axis_size((ATOM_OUTER, ATOM_PAIR, ATOM_CORE))
    zrows = QZ // lax.axis_size("loops")
    atom_total = position.shape[1] * group_count
    zfirst = (lax.axis_index("loops") * zrows).astype(jnp.float32)
    zwaves = waves(zfirst, zrows, QZ, 0.0)
    ywaves = waves(jnp.float32(0.0), QY, QY, 1.0)
    xwaves = waves(jnp.float32(0.0), QX, QX, 1.0)
    zcosines, zsines, ytable = phase_tables(position, ywaves, zwaves)
    outer = lax.axis_size(ATOM_OUTER)
    core = lax.axis_index(ATOM_CORE)
    pair = lax.axis_index(ATOM_PAIR)
    block = QX // (4 * outer)
    run = jnp.arange(block, dtype=jnp.int32)

    def rows(fine_picked):
        tables = sincos_rows(*steps_of(xwaves, fine_picked), position[0], fine_major=True)
        return factor_block(*tables, zcosines, zsines, ytable)

    for_core = jnp.concatenate([run, run + 2 * block]) + block * (1 - core)
    arrived = lax.ppermute(rows(for_core), ATOM_CORE, [(0, 1), (1, 0)])
    arrived = arrived.reshape(2, -1, *arrived.shape[1:])
    mine = 2 * block * pair + block * core
    away = rows(2 * block * (1 - pair) + block * core + run)
    away = away + lax.dynamic_index_in_dim(arrived, 1 - pair, axis=0, keepdims=False)
    away, kept_picked = lax.optimization_barrier((away, mine + run))
    returned = lax.ppermute(away, ATOM_PAIR, [(0, 1), (1, 0)])
    kept = rows(kept_picked)
    kept = kept + lax.dynamic_index_in_dim(arrived, pair, axis=0, keepdims=False)
    partial = kept + returned
    blocks = partial.reshape(block, outer, *partial.shape[1:])
    summed = lax.all_to_all(blocks, ATOM_OUTER, 1, 1, tiled=True).sum(axis=1)
    power = summed[:, 0] ** 2 + summed[:, 1] ** 2
    return jnp.log1p(jnp.transpose(power, (1, 0, 2)) / atom_total)


ATOM_OUTER = "atom_outer"
ATOM_PAIR = "atom_pair"
ATOM_CORE = "atom_core"


def solution(mesh):
    groups, loop_groups = mesh.devices.shape
    split = Mesh(
        mesh.devices.reshape(groups // 4, 2, 2, loop_groups),
        (ATOM_OUTER, ATOM_PAIR, ATOM_CORE, "loops"),
    )
    atoms = (ATOM_OUTER, ATOM_PAIR, ATOM_CORE)
    placed = (P(atoms), P(None, "loops"), P("loops"), P("loops"), P("loops"))
    return jax.shard_map(
        body, mesh=split, in_specs=placed, out_specs=P("loops", atoms, None), check_vma=False
    )
```

```python
import math

import jax
import jax.numpy as jnp
import numpy as np
from jax import lax
from jax.experimental import pallas as pl
from jax.experimental.pallas import tpu as pltpu
from jax.sharding import Mesh, PartitionSpec as P

WIN_X = 32
WIN_Y = 32
QX = 128
QY = 128
QZ = 64


LATTICE = 2.8665
POISSON = 0.29
TWO_PI = 2.0 * math.pi
BURGERS_TABLE = np.array(
    [[1.0, 1.0, 1.0], [-1.0, 1.0, 1.0], [1.0, -1.0, 1.0], [1.0, 1.0, -1.0]]
) * (0.5 * LATTICE)
NORMAL_TABLE = (
    np.array(
        [
            [1.0, 1.0, 0.0],
            [1.0, -1.0, 0.0],
            [1.0, 0.0, 1.0],
            [1.0, 0.0, -1.0],
            [0.0, 1.0, 1.0],
            [0.0, 1.0, -1.0],
        ]
    )
    * 0.70710678
)


def lookup(index, table):
    columns = []
    for column in range(3):
        total = jnp.zeros(index.shape, jnp.float32)
        for entry in range(table.shape[0]):
            total = total + jnp.where(
                index == entry, jnp.float32(table[entry, column]), jnp.float32(0.0)
            )
        columns.append(total)
    return jnp.stack(columns)


def site_anchor(site):
    basis = site % 2
    cell = site // 2
    first = cell % WIN_X
    second = cell // WIN_X % WIN_Y
    third = cell // (WIN_X * WIN_Y)
    cells = jnp.stack([first, second, third]).astype(jnp.float32)
    return LATTICE * (cells + 0.5 * basis.astype(jnp.float32)[None, :])


def loop_centre(cells):
    return LATTICE * (cells.astype(jnp.float32) + 0.25)


def loop_field(anchor, centre, burgers, normal, radius):
    offset = anchor[:, None, :] - centre[:, :, None]
    radius_sq = (radius * radius)[:, None]
    distance_sq = jnp.sum(offset * offset, axis=0) + radius_sq
    unit_dir = offset * lax.rsqrt(distance_sq)[None]
    along_b = jnp.sum(burgers[:, :, None] * unit_dir, axis=0)
    along_n = jnp.sum(normal[:, :, None] * unit_dir, axis=0)
    burgers_normal = jnp.sum(burgers * normal, axis=0)[:, None]
    strength = radius_sq / (8.0 * (1.0 - POISSON) * distance_sq)
    field = (1.0 - 2.0 * POISSON) * (
        burgers[:, :, None] * along_n[None] + normal[:, :, None] * along_b[None]
    )
    field = field - burgers_normal[None] * unit_dir + 3.0 * unit_dir * (along_b * along_n)[None]
    return jnp.sum(strength[None] * field, axis=1)


def waves(first, count, total, centre):
    steps = first + jnp.arange(count, dtype=jnp.float32)
    return TWO_PI / LATTICE * (centre + (steps - total * 0.5 + 0.5) / QX)


def factor_block(xcosines, xsines, zcosines, zsines, ytable):
    ywidth = ytable.shape[0] // 2
    left_real = (
        zcosines[None, :, :] * xcosines[:, None, :] - zsines[None, :, :] * xsines[:, None, :]
    )
    left_imag = (
        zcosines[None, :, :] * xsines[:, None, :] + zsines[None, :, :] * xcosines[:, None, :]
    )
    left_pair = jnp.stack([left_real, left_imag], axis=2)
    product = jnp.einsum(
        "xzca,da->xzcd",
        left_pair,
        ytable,
        precision=lax.Precision.HIGH,
        preferred_element_type=jnp.float32,
    )
    real_part = product[:, :, 0, :ywidth] - product[:, :, 1, ywidth:]
    imag_part = product[:, :, 0, ywidth:] + product[:, :, 1, :ywidth]
    return jnp.stack([real_part, imag_part], axis=1)


FINE_STEPS = 16


def sincos_rows(coarse, fine, values):
    coarse_angle = coarse[:, None] * values[None, :]
    fine_angle = fine[:, None] * values[None, :]
    cc, sc = jnp.cos(coarse_angle), jnp.sin(coarse_angle)
    cf, sf = jnp.cos(fine_angle), jnp.sin(fine_angle)
    cosines = cc[:, None, :] * cf[None, :, :] - sc[:, None, :] * sf[None, :, :]
    sines = sc[:, None, :] * cf[None, :, :] + cc[:, None, :] * sf[None, :, :]
    shape = (coarse.shape[0] * fine.shape[0], values.shape[0])
    return cosines.reshape(shape), sines.reshape(shape)


def steps_of(waves_row, picked=None):
    fine = waves_row[:FINE_STEPS] - waves_row[0]
    if picked is not None:
        fine = jnp.take(fine, picked)
    return waves_row[::FINE_STEPS], fine


def phase_tables(position, ywaves, zwaves):
    ycosines, ysines = sincos_rows(*steps_of(ywaves), position[1])
    zangle = zwaves[:, None] * position[2][None, :]
    ytable = jnp.concatenate([ycosines, ysines], axis=0)
    return jnp.cos(zangle), jnp.sin(zangle), ytable


HALF_BURGERS = float(BURGERS_TABLE[0, 0])
HABIT_SCALE = float(NORMAL_TABLE[0, 0])
STRENGTH_SCALE = 1.0 / (8.0 * (1.0 - POISSON))
FIELD_SPLIT = 2
FIELD_UNROLL = 2


def field_kernel(cells, burgers_index, habit_index, radius, site, anchor_out, field_out):
    whole = site[...]
    basis = jnp.bitwise_and(whole, 1)
    cell = jnp.right_shift(whole, 1)
    first = jnp.bitwise_and(cell, WIN_X - 1)
    second = jnp.bitwise_and(jnp.right_shift(cell, 5), WIN_Y - 1)
    third = jnp.right_shift(cell, 10)
    half = 0.5 * basis.astype(jnp.float32)
    coords = [LATTICE * (c.astype(jnp.float32) + half) for c in (first, second, third)]
    for axis in range(3):
        anchor_out[axis] = coords[axis]
    rows = whole.shape[0] // FIELD_SPLIT
    pieces = [[c[p * rows : (p + 1) * rows] for c in coords] for p in range(FIELD_SPLIT)]

    def one_loop(number, running):
        cx = LATTICE * (cells[0, number].astype(jnp.float32) + 0.25)
        cy = LATTICE * (cells[1, number].astype(jnp.float32) + 0.25)
        cz = LATTICE * (cells[2, number].astype(jnp.float32) + 0.25)
        kb = burgers_index[number]
        kh = habit_index[number]
        h = jnp.float32(HALF_BURGERS)
        bx = jnp.where(kb == 1, -h, h)
        by = jnp.where(kb == 2, -h, h)
        bz = jnp.where(kb == 3, -h, h)
        c = jnp.float32(HABIT_SCALE)
        zero = jnp.float32(0.0)
        nx = jnp.where(kh < 4, c, zero)
        ny = jnp.where(kh == 1, -c, jnp.where((kh == 2) | (kh == 3), zero, c))
        nz = jnp.where((kh == 2) | (kh == 4), c, jnp.where((kh == 3) | (kh == 5), -c, zero))
        burgers_normal = bx * nx + by * ny + bz * nz
        r = radius[number]
        radius_sq = r * r
        scale = radius_sq * jnp.float32(STRENGTH_SCALE)
        scaled_b = [jnp.float32(1.0 - 2.0 * POISSON) * v for v in (bx, by, bz)]
        scaled_n = [jnp.float32(1.0 - 2.0 * POISSON) * v for v in (nx, ny, nz)]
        out = []
        for p in range(FIELD_SPLIT):
            ax, ay, az = pieces[p]
            dx, dy, dz = ax - cx, ay - cy, az - cz
            distance_sq = dx * dx + dy * dy + dz * dz + radius_sq
            inverse = lax.rsqrt(distance_sq)
            inverse_sq = inverse * inverse
            toward_b = bx * dx + by * dy + bz * dz
            toward_n = nx * dx + ny * dy + nz * dz
            weight = scale * (inverse_sq * inverse)
            mixed = (3.0 * inverse_sq) * (toward_b * toward_n) - burgers_normal
            on_n = weight * toward_n
            on_b = weight * toward_b
            on_d = weight * mixed
            out.append(
                tuple(
                    total + (sb * on_n + sn * on_b + d * on_d)
                    for total, sb, sn, d in zip(running[p], scaled_b, scaled_n, (dx, dy, dz))
                )
            )
        return tuple(out)

    zero = jnp.zeros((rows, whole.shape[1]), jnp.float32)
    start = tuple((zero, zero, zero) for _ in range(FIELD_SPLIT))
    totals = lax.fori_loop(0, radius.shape[0], one_loop, start, unroll=FIELD_UNROLL)
    for p in range(FIELD_SPLIT):
        for axis in range(3):
            field_out[axis, p * rows : (p + 1) * rows] = totals[p][axis]


def anchor_and_field(atom_site, loop_cells, loop_burgers, loop_habit, loop_radius):
    atoms = atom_site.shape[0]
    loops = loop_radius.shape[0]
    tiled = atom_site.reshape(atoms // 128, 128)
    smem = pl.BlockSpec(memory_space=pltpu.SMEM)
    vmem = pl.BlockSpec(memory_space=pltpu.VMEM)
    shape = jax.ShapeDtypeStruct((3, *tiled.shape), jnp.float32)
    anchor, field = pl.pallas_call(
        field_kernel,
        in_specs=[smem, smem, smem, smem, vmem],
        out_specs=[vmem, vmem],
        out_shape=[shape, shape],
        cost_estimate=pl.CostEstimate(
            flops=55 * atoms * loops, transcendentals=atoms * loops, bytes_accessed=28 * atoms
        ),
    )(loop_cells, loop_burgers, loop_habit, loop_radius, tiled)
    return anchor.reshape(3, atoms), field

def body(atom_site, loop_cells, loop_burgers, loop_habit, loop_radius):
    anchor, field = anchor_and_field(atom_site, loop_cells, loop_burgers, loop_habit, loop_radius)
    loop_groups = lax.axis_size("loops")
    rows = field.shape[1] // loop_groups
    owned = lax.all_to_all(
        field.reshape(3, loop_groups, rows, field.shape[2]), "loops", 1, 1, tiled=True
    ).sum(axis=1)
    displacement = lax.all_to_all(
        jnp.broadcast_to(owned[:, None], (3, loop_groups, *owned.shape[1:])), "loops", 1, 1, tiled=True
    ).reshape(3, -1)
    position = anchor + displacement
    group_count = lax.axis_size((ATOM_OUTER, ATOM_CORE))
    zrows = QZ // lax.axis_size("loops")
    atom_total = position.shape[1] * group_count
    zfirst = (lax.axis_index("loops") * zrows).astype(jnp.float32)
    zwaves = waves(zfirst, zrows, QZ, 0.0)
    ywaves = waves(jnp.float32(0.0), QY, QY, 1.0)
    xwaves = waves(jnp.float32(0.0), QX, QX, 1.0)
    zcosines, zsines, ytable = phase_tables(position, ywaves, zwaves)
    outer = lax.axis_size(ATOM_OUTER)
    core = lax.axis_index(ATOM_CORE)
    block = QX // (2 * outer)
    lanes = np.arange(FINE_STEPS)
    first_side = jnp.asarray(lanes[(lanes // block) % 2 == 0], jnp.int32)

    def half(side):
        xcosines, xsines = sincos_rows(*steps_of(xwaves, first_side + block * side), position[0])
        return factor_block(xcosines, xsines, zcosines, zsines, ytable)

    sent = half(1 - core)
    arrived = lax.ppermute(sent, ATOM_CORE, [(0, 1), (1, 0)])
    kept = half(core)
    partial = kept + arrived
    blocks = partial.reshape(outer, -1, *partial.shape[1:])
    summed = lax.all_to_all(blocks, ATOM_OUTER, 0, 0, tiled=True).sum(axis=0)
    power = summed[:, 0] ** 2 + summed[:, 1] ** 2
    return jnp.log1p(jnp.transpose(power, (1, 0, 2)) / atom_total)


ATOM_OUTER = "atom_pairs"
ATOM_CORE = "atom_core"


def solution(mesh):
    groups, loop_groups = mesh.devices.shape
    paired = Mesh(
        mesh.devices.reshape(groups // 2, 2, loop_groups), (ATOM_OUTER, ATOM_CORE, "loops")
    )
    atoms = (ATOM_OUTER, ATOM_CORE)
    placed = (P(atoms), P(None, "loops"), P("loops"), P("loops"), P("loops"))
    return jax.shard_map(
        body, mesh=paired, in_specs=placed, out_specs=P("loops", atoms, None), check_vma=False
    )
```

```python
import math

import jax
import jax.numpy as jnp
import numpy as np
from jax import lax
from jax.experimental import pallas as pl
from jax.experimental.pallas import tpu as pltpu
from jax.sharding import Mesh, PartitionSpec as P

WIN_X = 32
WIN_Y = 32
QX = 128
QY = 128
QZ = 64


LATTICE = 2.8665
POISSON = 0.29
TWO_PI = 2.0 * math.pi
BURGERS_TABLE = np.array(
    [[1.0, 1.0, 1.0], [-1.0, 1.0, 1.0], [1.0, -1.0, 1.0], [1.0, 1.0, -1.0]]
) * (0.5 * LATTICE)
NORMAL_TABLE = (
    np.array(
        [
            [1.0, 1.0, 0.0],
            [1.0, -1.0, 0.0],
            [1.0, 0.0, 1.0],
            [1.0, 0.0, -1.0],
            [0.0, 1.0, 1.0],
            [0.0, 1.0, -1.0],
        ]
    )
    * 0.70710678
)


def lookup(index, table):
    columns = []
    for column in range(3):
        total = jnp.zeros(index.shape, jnp.float32)
        for entry in range(table.shape[0]):
            total = total + jnp.where(
                index == entry, jnp.float32(table[entry, column]), jnp.float32(0.0)
            )
        columns.append(total)
    return jnp.stack(columns)


def site_anchor(site):
    basis = site % 2
    cell = site // 2
    first = cell % WIN_X
    second = cell // WIN_X % WIN_Y
    third = cell // (WIN_X * WIN_Y)
    cells = jnp.stack([first, second, third]).astype(jnp.float32)
    return LATTICE * (cells + 0.5 * basis.astype(jnp.float32)[None, :])


def loop_centre(cells):
    return LATTICE * (cells.astype(jnp.float32) + 0.25)


def loop_field(anchor, centre, burgers, normal, radius):
    offset = anchor[:, None, :] - centre[:, :, None]
    radius_sq = (radius * radius)[:, None]
    distance_sq = jnp.sum(offset * offset, axis=0) + radius_sq
    unit_dir = offset * lax.rsqrt(distance_sq)[None]
    along_b = jnp.sum(burgers[:, :, None] * unit_dir, axis=0)
    along_n = jnp.sum(normal[:, :, None] * unit_dir, axis=0)
    burgers_normal = jnp.sum(burgers * normal, axis=0)[:, None]
    strength = radius_sq / (8.0 * (1.0 - POISSON) * distance_sq)
    field = (1.0 - 2.0 * POISSON) * (
        burgers[:, :, None] * along_n[None] + normal[:, :, None] * along_b[None]
    )
    field = field - burgers_normal[None] * unit_dir + 3.0 * unit_dir * (along_b * along_n)[None]
    return jnp.sum(strength[None] * field, axis=1)


def waves(first, count, total, centre):
    steps = first + jnp.arange(count, dtype=jnp.float32)
    return TWO_PI / LATTICE * (centre + (steps - total * 0.5 + 0.5) / QX)


def factor_block(xcosines, xsines, zcosines, zsines, ytable):
    left_real = (
        zcosines[None, :, :] * xcosines[:, None, :] - zsines[None, :, :] * xsines[:, None, :]
    )
    left_imag = (
        zcosines[None, :, :] * xsines[:, None, :] + zsines[None, :, :] * xcosines[:, None, :]
    )
    left_three = jnp.stack([left_real + left_imag, left_real, left_imag])
    product = jnp.einsum(
        "gxza,gda->gxzd",
        left_three,
        ytable,
        precision=lax.Precision.HIGH,
        preferred_element_type=jnp.float32,
    )
    real_part = product[0] - product[2]
    imag_part = product[0] + product[1]
    return jnp.stack([real_part, imag_part], axis=1)


FINE_STEPS = 16


def sincos_rows(coarse, fine, values):
    coarse_angle = coarse[:, None] * values[None, :]
    fine_angle = fine[:, None] * values[None, :]
    cc, sc = jnp.cos(coarse_angle), jnp.sin(coarse_angle)
    cf, sf = jnp.cos(fine_angle), jnp.sin(fine_angle)
    cosines = cc[:, None, :] * cf[None, :, :] - sc[:, None, :] * sf[None, :, :]
    sines = sc[:, None, :] * cf[None, :, :] + cc[:, None, :] * sf[None, :, :]
    shape = (coarse.shape[0] * fine.shape[0], values.shape[0])
    return cosines.reshape(shape), sines.reshape(shape)


def steps_of(waves_row, picked=None):
    fine = waves_row[:FINE_STEPS] - waves_row[0]
    if picked is not None:
        fine = jnp.take(fine, picked)
    return waves_row[::FINE_STEPS], fine


def phase_tables(position, ywaves, zwaves):
    ycosines, ysines = sincos_rows(*steps_of(ywaves), position[1])
    zangle = zwaves[:, None] * position[2][None, :]
    ytable = jnp.stack([ycosines, ysines - ycosines, ycosines + ysines])
    return jnp.cos(zangle), jnp.sin(zangle), ytable


HALF_BURGERS = float(BURGERS_TABLE[0, 0])
HABIT_SCALE = float(NORMAL_TABLE[0, 0])
STRENGTH_SCALE = 1.0 / (8.0 * (1.0 - POISSON))
FIELD_SPLIT = 2
FIELD_UNROLL = 2


def field_kernel(cells, burgers_index, habit_index, radius, site, anchor_out, field_out):
    whole = site[...]
    basis = jnp.bitwise_and(whole, 1)
    cell = jnp.right_shift(whole, 1)
    first = jnp.bitwise_and(cell, WIN_X - 1)
    second = jnp.bitwise_and(jnp.right_shift(cell, 5), WIN_Y - 1)
    third = jnp.right_shift(cell, 10)
    half = 0.5 * basis.astype(jnp.float32)
    coords = [LATTICE * (c.astype(jnp.float32) + half) for c in (first, second, third)]
    for axis in range(3):
        anchor_out[axis] = coords[axis]
    rows = whole.shape[0] // FIELD_SPLIT
    pieces = [[c[p * rows : (p + 1) * rows] for c in coords] for p in range(FIELD_SPLIT)]

    def one_loop(number, running):
        cx = LATTICE * (cells[0, number].astype(jnp.float32) + 0.25)
        cy = LATTICE * (cells[1, number].astype(jnp.float32) + 0.25)
        cz = LATTICE * (cells[2, number].astype(jnp.float32) + 0.25)
        kb = burgers_index[number]
        kh = habit_index[number]
        h = jnp.float32(HALF_BURGERS)
        bx = jnp.where(kb == 1, -h, h)
        by = jnp.where(kb == 2, -h, h)
        bz = jnp.where(kb == 3, -h, h)
        c = jnp.float32(HABIT_SCALE)
        zero = jnp.float32(0.0)
        nx = jnp.where(kh < 4, c, zero)
        ny = jnp.where(kh == 1, -c, jnp.where((kh == 2) | (kh == 3), zero, c))
        nz = jnp.where((kh == 2) | (kh == 4), c, jnp.where((kh == 3) | (kh == 5), -c, zero))
        burgers_normal = bx * nx + by * ny + bz * nz
        r = radius[number]
        radius_sq = r * r
        scale = radius_sq * jnp.float32(STRENGTH_SCALE)
        scaled_b = [jnp.float32(1.0 - 2.0 * POISSON) * v for v in (bx, by, bz)]
        scaled_n = [jnp.float32(1.0 - 2.0 * POISSON) * v for v in (nx, ny, nz)]
        out = []
        for p in range(FIELD_SPLIT):
            ax, ay, az = pieces[p]
            dx, dy, dz = ax - cx, ay - cy, az - cz
            distance_sq = dx * dx + dy * dy + dz * dz + radius_sq
            inverse = lax.rsqrt(distance_sq)
            inverse_sq = inverse * inverse
            toward_b = bx * dx + by * dy + bz * dz
            toward_n = nx * dx + ny * dy + nz * dz
            weight = scale * (inverse_sq * inverse)
            mixed = (3.0 * inverse_sq) * (toward_b * toward_n) - burgers_normal
            on_n = weight * toward_n
            on_b = weight * toward_b
            on_d = weight * mixed
            out.append(
                tuple(
                    total + (sb * on_n + sn * on_b + d * on_d)
                    for total, sb, sn, d in zip(running[p], scaled_b, scaled_n, (dx, dy, dz))
                )
            )
        return tuple(out)

    zero = jnp.zeros((rows, whole.shape[1]), jnp.float32)
    start = tuple((zero, zero, zero) for _ in range(FIELD_SPLIT))
    totals = lax.fori_loop(0, radius.shape[0], one_loop, start, unroll=FIELD_UNROLL)
    for p in range(FIELD_SPLIT):
        for axis in range(3):
            field_out[axis, p * rows : (p + 1) * rows] = totals[p][axis]


def anchor_and_field(atom_site, loop_cells, loop_burgers, loop_habit, loop_radius):
    atoms = atom_site.shape[0]
    loops = loop_radius.shape[0]
    tiled = atom_site.reshape(atoms // 128, 128)
    smem = pl.BlockSpec(memory_space=pltpu.SMEM)
    vmem = pl.BlockSpec(memory_space=pltpu.VMEM)
    shape = jax.ShapeDtypeStruct((3, *tiled.shape), jnp.float32)
    anchor, field = pl.pallas_call(
        field_kernel,
        in_specs=[smem, smem, smem, smem, vmem],
        out_specs=[vmem, vmem],
        out_shape=[shape, shape],
        cost_estimate=pl.CostEstimate(
            flops=55 * atoms * loops, transcendentals=atoms * loops, bytes_accessed=28 * atoms
        ),
    )(loop_cells, loop_burgers, loop_habit, loop_radius, tiled)
    return anchor.reshape(3, atoms), field

def body(atom_site, loop_cells, loop_burgers, loop_habit, loop_radius):
    anchor, field = anchor_and_field(atom_site, loop_cells, loop_burgers, loop_habit, loop_radius)
    loop_groups = lax.axis_size("loops")
    rows = field.shape[1] // loop_groups
    owned = lax.all_to_all(
        field.reshape(3, loop_groups, rows, field.shape[2]), "loops", 1, 1, tiled=True
    ).sum(axis=1)
    displacement = lax.all_to_all(
        jnp.broadcast_to(owned[:, None], (3, loop_groups, *owned.shape[1:])), "loops", 1, 1, tiled=True
    ).reshape(3, -1)
    position = anchor + displacement
    group_count = lax.axis_size((ATOM_OUTER, ATOM_CORE))
    zrows = QZ // lax.axis_size("loops")
    atom_total = position.shape[1] * group_count
    zfirst = (lax.axis_index("loops") * zrows).astype(jnp.float32)
    zwaves = waves(zfirst, zrows, QZ, 0.0)
    ywaves = waves(jnp.float32(0.0), QY, QY, 1.0)
    xwaves = waves(jnp.float32(0.0), QX, QX, 1.0)
    zcosines, zsines, ytable = phase_tables(position, ywaves, zwaves)
    outer = lax.axis_size(ATOM_OUTER)
    core = lax.axis_index(ATOM_CORE)
    block = QX // (2 * outer)
    lanes = np.arange(FINE_STEPS)
    first_side = jnp.asarray(lanes[(lanes // block) % 2 == 0], jnp.int32)

    def half(side):
        xcosines, xsines = sincos_rows(*steps_of(xwaves, first_side + block * side), position[0])
        return factor_block(xcosines, xsines, zcosines, zsines, ytable)

    sent = half(1 - core)
    arrived = lax.ppermute(sent, ATOM_CORE, [(0, 1), (1, 0)])
    kept = half(core)
    partial = kept + arrived
    blocks = partial.reshape(outer, -1, *partial.shape[1:])
    summed = lax.all_to_all(blocks, ATOM_OUTER, 0, 0, tiled=True).sum(axis=0)
    power = summed[:, 0] ** 2 + summed[:, 1] ** 2
    return jnp.log1p(jnp.transpose(power, (1, 0, 2)) / atom_total)


ATOM_OUTER = "atom_pairs"
ATOM_CORE = "atom_core"


def solution(mesh):
    groups, loop_groups = mesh.devices.shape
    paired = Mesh(
        mesh.devices.reshape(groups // 2, 2, loop_groups), (ATOM_OUTER, ATOM_CORE, "loops")
    )
    atoms = (ATOM_OUTER, ATOM_CORE)
    placed = (P(atoms), P(None, "loops"), P("loops"), P("loops"), P("loops"))
    return jax.shard_map(
        body, mesh=paired, in_specs=placed, out_specs=P("loops", atoms, None), check_vma=False
    )
```

```python
import math

import jax
import jax.numpy as jnp
import numpy as np
from jax import lax
from jax.experimental import pallas as pl
from jax.experimental.pallas import tpu as pltpu
from jax.sharding import Mesh, PartitionSpec as P

WIN_X = 32
WIN_Y = 32
QX = 128
QY = 128
QZ = 64


LATTICE = 2.8665
POISSON = 0.29
TWO_PI = 2.0 * math.pi
BURGERS_TABLE = np.array(
    [[1.0, 1.0, 1.0], [-1.0, 1.0, 1.0], [1.0, -1.0, 1.0], [1.0, 1.0, -1.0]]
) * (0.5 * LATTICE)
NORMAL_TABLE = (
    np.array(
        [
            [1.0, 1.0, 0.0],
            [1.0, -1.0, 0.0],
            [1.0, 0.0, 1.0],
            [1.0, 0.0, -1.0],
            [0.0, 1.0, 1.0],
            [0.0, 1.0, -1.0],
        ]
    )
    * 0.70710678
)


def lookup(index, table):
    columns = []
    for column in range(3):
        total = jnp.zeros(index.shape, jnp.float32)
        for entry in range(table.shape[0]):
            total = total + jnp.where(
                index == entry, jnp.float32(table[entry, column]), jnp.float32(0.0)
            )
        columns.append(total)
    return jnp.stack(columns)


def site_anchor(site):
    basis = site % 2
    cell = site // 2
    first = cell % WIN_X
    second = cell // WIN_X % WIN_Y
    third = cell // (WIN_X * WIN_Y)
    cells = jnp.stack([first, second, third]).astype(jnp.float32)
    return LATTICE * (cells + 0.5 * basis.astype(jnp.float32)[None, :])


def loop_centre(cells):
    return LATTICE * (cells.astype(jnp.float32) + 0.25)


def loop_field(anchor, centre, burgers, normal, radius):
    offset = anchor[:, None, :] - centre[:, :, None]
    radius_sq = (radius * radius)[:, None]
    distance_sq = jnp.sum(offset * offset, axis=0) + radius_sq
    unit_dir = offset * lax.rsqrt(distance_sq)[None]
    along_b = jnp.sum(burgers[:, :, None] * unit_dir, axis=0)
    along_n = jnp.sum(normal[:, :, None] * unit_dir, axis=0)
    burgers_normal = jnp.sum(burgers * normal, axis=0)[:, None]
    strength = radius_sq / (8.0 * (1.0 - POISSON) * distance_sq)
    field = (1.0 - 2.0 * POISSON) * (
        burgers[:, :, None] * along_n[None] + normal[:, :, None] * along_b[None]
    )
    field = field - burgers_normal[None] * unit_dir + 3.0 * unit_dir * (along_b * along_n)[None]
    return jnp.sum(strength[None] * field, axis=1)


def waves(first, count, total, centre):
    steps = first + jnp.arange(count, dtype=jnp.float32)
    return TWO_PI / LATTICE * (centre + (steps - total * 0.5 + 0.5) / QX)


def factor_block(xcosines, xsines, zcosines, zsines, ytable):
    ywidth = ytable.shape[0] // 2
    left_real = (
        zcosines[None, :, :] * xcosines[:, None, :] - zsines[None, :, :] * xsines[:, None, :]
    )
    left_imag = (
        zcosines[None, :, :] * xsines[:, None, :] + zsines[None, :, :] * xcosines[:, None, :]
    )
    left_pair = jnp.stack([left_real, left_imag], axis=2)
    product = jnp.einsum(
        "xzca,da->xzcd",
        left_pair,
        ytable,
        precision=lax.Precision.HIGH,
        preferred_element_type=jnp.float32,
    )
    real_part = product[:, :, 0, :ywidth] - product[:, :, 1, ywidth:]
    imag_part = product[:, :, 0, ywidth:] + product[:, :, 1, :ywidth]
    return jnp.stack([real_part, imag_part], axis=1)


FINE_STEPS = 16


def sincos_rows(coarse, fine, values):
    coarse_angle = coarse[:, None] * values[None, :]
    fine_angle = fine[:, None] * values[None, :]
    cc, sc = jnp.cos(coarse_angle), jnp.sin(coarse_angle)
    cf, sf = jnp.cos(fine_angle), jnp.sin(fine_angle)
    cosines = cc[:, None, :] * cf[None, :, :] - sc[:, None, :] * sf[None, :, :]
    sines = sc[:, None, :] * cf[None, :, :] + cc[:, None, :] * sf[None, :, :]
    shape = (coarse.shape[0] * fine.shape[0], values.shape[0])
    return cosines.reshape(shape), sines.reshape(shape)


def steps_of(waves_row, picked=None):
    fine = waves_row[:FINE_STEPS] - waves_row[0]
    if picked is not None:
        fine = jnp.take(fine, picked)
    return waves_row[::FINE_STEPS], fine


def phase_tables(position, ywaves, zwaves):
    ycosines, ysines = sincos_rows(*steps_of(ywaves), position[1])
    zangle = zwaves[:, None] * position[2][None, :]
    ytable = jnp.concatenate([ycosines, ysines], axis=0)
    return jnp.cos(zangle), jnp.sin(zangle), ytable


HALF_BURGERS = float(BURGERS_TABLE[0, 0])
HABIT_SCALE = float(NORMAL_TABLE[0, 0])
STRENGTH_SCALE = 1.0 / (8.0 * (1.0 - POISSON))
FIELD_SPLIT = 2
FIELD_UNROLL = 2
FIELD_SLOTS = 8


def field_kernel(cells, burgers_index, habit_index, radius, site, anchor_out, field_out):
    whole = site[...]
    basis = jnp.bitwise_and(whole, 1)
    cell = jnp.right_shift(whole, 1)
    first = jnp.bitwise_and(cell, WIN_X - 1)
    second = jnp.bitwise_and(jnp.right_shift(cell, 5), WIN_Y - 1)
    third = jnp.right_shift(cell, 10)
    half = 0.5 * basis.astype(jnp.float32)
    coords = [LATTICE * (c.astype(jnp.float32) + half) for c in (first, second, third)]
    for axis in range(3):
        anchor_out[axis] = coords[axis]
    rows = whole.shape[0] // FIELD_SPLIT
    pieces = [[c[p * rows : (p + 1) * rows] for c in coords] for p in range(FIELD_SPLIT)]

    def one_loop(number, running):
        cx = LATTICE * (cells[0, number].astype(jnp.float32) + 0.25)
        cy = LATTICE * (cells[1, number].astype(jnp.float32) + 0.25)
        cz = LATTICE * (cells[2, number].astype(jnp.float32) + 0.25)
        kb = burgers_index[number]
        kh = habit_index[number]
        h = jnp.float32(HALF_BURGERS)
        bx = jnp.where(kb == 1, -h, h)
        by = jnp.where(kb == 2, -h, h)
        bz = jnp.where(kb == 3, -h, h)
        c = jnp.float32(HABIT_SCALE)
        zero = jnp.float32(0.0)
        nx = jnp.where(kh < 4, c, zero)
        ny = jnp.where(kh == 1, -c, jnp.where((kh == 2) | (kh == 3), zero, c))
        nz = jnp.where((kh == 2) | (kh == 4), c, jnp.where((kh == 3) | (kh == 5), -c, zero))
        burgers_normal = bx * nx + by * ny + bz * nz
        r = radius[number]
        radius_sq = r * r
        scale = radius_sq * jnp.float32(STRENGTH_SCALE)
        scaled_b = [jnp.float32(1.0 - 2.0 * POISSON) * v for v in (bx, by, bz)]
        scaled_n = [jnp.float32(1.0 - 2.0 * POISSON) * v for v in (nx, ny, nz)]
        out = []
        for p in range(FIELD_SPLIT):
            ax, ay, az = pieces[p]
            dx, dy, dz = ax - cx, ay - cy, az - cz
            distance_sq = dx * dx + dy * dy + dz * dz + radius_sq
            inverse = lax.rsqrt(distance_sq)
            inverse_sq = inverse * inverse
            toward_b = bx * dx + by * dy + bz * dz
            toward_n = nx * dx + ny * dy + nz * dz
            weight = scale * (inverse_sq * inverse)
            mixed = (3.0 * inverse_sq) * (toward_b * toward_n) - burgers_normal
            on_n = weight * toward_n
            on_b = weight * toward_b
            on_d = weight * mixed
            out.append(
                tuple(
                    total + (sb * on_n + sn * on_b + d * on_d)
                    for total, sb, sn, d in zip(running[p], scaled_b, scaled_n, (dx, dy, dz))
                )
            )
        return tuple(out)

    zero = jnp.zeros((rows, whole.shape[1]), jnp.float32)
    start = tuple((zero, zero, zero) for _ in range(FIELD_SPLIT))
    totals = lax.fori_loop(0, radius.shape[0], one_loop, start, unroll=FIELD_UNROLL)
    slots = field_out.shape[0] // rows
    for p in range(FIELD_SPLIT):
        for axis in range(3):
            field_out[pl.ds(axis * FIELD_SPLIT + p, rows, stride=slots), :] = totals[p][axis]
    spare = jnp.zeros((rows, whole.shape[1]), jnp.float32)
    for slot in range(3 * FIELD_SPLIT, slots):
        field_out[pl.ds(slot, rows, stride=slots), :] = spare


def anchor_and_field(atom_site, loop_cells, loop_burgers, loop_habit, loop_radius):
    atoms = atom_site.shape[0]
    loops = loop_radius.shape[0]
    tiled = atom_site.reshape(atoms // 128, 128)
    smem = pl.BlockSpec(memory_space=pltpu.SMEM)
    vmem = pl.BlockSpec(memory_space=pltpu.VMEM)
    shape = jax.ShapeDtypeStruct((3, *tiled.shape), jnp.float32)
    rows = tiled.shape[0] // FIELD_SPLIT
    chunked = jax.ShapeDtypeStruct((rows * FIELD_SLOTS, 128), jnp.float32)
    anchor, field = pl.pallas_call(
        field_kernel,
        in_specs=[smem, smem, smem, smem, vmem],
        out_specs=[vmem, vmem],
        out_shape=[shape, chunked],
        cost_estimate=pl.CostEstimate(
            flops=55 * atoms * loops, transcendentals=atoms * loops, bytes_accessed=28 * atoms
        ),
    )(loop_cells, loop_burgers, loop_habit, loop_radius, tiled)
    return anchor.reshape(3, atoms), field

def body(atom_site, loop_cells, loop_burgers, loop_habit, loop_radius):
    anchor, field = anchor_and_field(atom_site, loop_cells, loop_burgers, loop_habit, loop_radius)
    loop_groups = lax.axis_size("loops")
    chunks = field.reshape(loop_groups, FIELD_SLOTS, field.shape[1])
    owned = lax.all_to_all(chunks, "loops", 0, 0, tiled=True).sum(axis=0)
    gathered = lax.all_to_all(
        jnp.broadcast_to(owned[None], chunks.shape), "loops", 0, 0, tiled=True
    )
    used = gathered[:, : 3 * FIELD_SPLIT].reshape(loop_groups, 3, FIELD_SPLIT, field.shape[1])
    displacement = used.transpose(1, 2, 0, 3).reshape(3, -1)
    position = anchor + displacement
    group_count = lax.axis_size((ATOM_OUTER, ATOM_CORE))
    zrows = QZ // lax.axis_size("loops")
    atom_total = position.shape[1] * group_count
    zfirst = (lax.axis_index("loops") * zrows).astype(jnp.float32)
    zwaves = waves(zfirst, zrows, QZ, 0.0)
    ywaves = waves(jnp.float32(0.0), QY, QY, 1.0)
    xwaves = waves(jnp.float32(0.0), QX, QX, 1.0)
    zcosines, zsines, ytable = phase_tables(position, ywaves, zwaves)
    outer = lax.axis_size(ATOM_OUTER)
    core = lax.axis_index(ATOM_CORE)
    block = QX // (2 * outer)
    lanes = np.arange(FINE_STEPS)
    first_side = jnp.asarray(lanes[(lanes // block) % 2 == 0], jnp.int32)

    def half(side):
        xcosines, xsines = sincos_rows(*steps_of(xwaves, first_side + block * side), position[0])
        return factor_block(xcosines, xsines, zcosines, zsines, ytable)

    sent = half(1 - core)
    arrived = lax.ppermute(sent, ATOM_CORE, [(0, 1), (1, 0)])
    kept = half(core)
    partial = kept + arrived
    blocks = partial.reshape(outer, -1, *partial.shape[1:])
    summed = lax.all_to_all(blocks, ATOM_OUTER, 0, 0, tiled=True).sum(axis=0)
    power = summed[:, 0] ** 2 + summed[:, 1] ** 2
    return jnp.log1p(jnp.transpose(power, (1, 0, 2)) / atom_total)


ATOM_OUTER = "atom_pairs"
ATOM_CORE = "atom_core"


def solution(mesh):
    groups, loop_groups = mesh.devices.shape
    paired = Mesh(
        mesh.devices.reshape(groups // 2, 2, loop_groups), (ATOM_OUTER, ATOM_CORE, "loops")
    )
    atoms = (ATOM_OUTER, ATOM_CORE)
    placed = (P(atoms), P(None, "loops"), P("loops"), P("loops"), P("loops"))
    return jax.shard_map(
        body, mesh=paired, in_specs=placed, out_specs=P("loops", atoms, None), check_vma=False
    )
```

```python
import math

import jax
import jax.numpy as jnp
import numpy as np
from jax import lax
from jax.experimental import pallas as pl
from jax.experimental.pallas import tpu as pltpu
from jax.sharding import Mesh, PartitionSpec as P

WIN_X = 32
WIN_Y = 32
QX = 128
QY = 128
QZ = 64


LATTICE = 2.8665
POISSON = 0.29
TWO_PI = 2.0 * math.pi
BURGERS_TABLE = np.array(
    [[1.0, 1.0, 1.0], [-1.0, 1.0, 1.0], [1.0, -1.0, 1.0], [1.0, 1.0, -1.0]]
) * (0.5 * LATTICE)
NORMAL_TABLE = (
    np.array(
        [
            [1.0, 1.0, 0.0],
            [1.0, -1.0, 0.0],
            [1.0, 0.0, 1.0],
            [1.0, 0.0, -1.0],
            [0.0, 1.0, 1.0],
            [0.0, 1.0, -1.0],
        ]
    )
    * 0.70710678
)


def lookup(index, table):
    columns = []
    for column in range(3):
        total = jnp.zeros(index.shape, jnp.float32)
        for entry in range(table.shape[0]):
            total = total + jnp.where(
                index == entry, jnp.float32(table[entry, column]), jnp.float32(0.0)
            )
        columns.append(total)
    return jnp.stack(columns)


def site_anchor(site):
    basis = site % 2
    cell = site // 2
    first = cell % WIN_X
    second = cell // WIN_X % WIN_Y
    third = cell // (WIN_X * WIN_Y)
    cells = jnp.stack([first, second, third]).astype(jnp.float32)
    return LATTICE * (cells + 0.5 * basis.astype(jnp.float32)[None, :])


def loop_centre(cells):
    return LATTICE * (cells.astype(jnp.float32) + 0.25)


def loop_field(anchor, centre, burgers, normal, radius):
    offset = anchor[:, None, :] - centre[:, :, None]
    radius_sq = (radius * radius)[:, None]
    distance_sq = jnp.sum(offset * offset, axis=0) + radius_sq
    unit_dir = offset * lax.rsqrt(distance_sq)[None]
    along_b = jnp.sum(burgers[:, :, None] * unit_dir, axis=0)
    along_n = jnp.sum(normal[:, :, None] * unit_dir, axis=0)
    burgers_normal = jnp.sum(burgers * normal, axis=0)[:, None]
    strength = radius_sq / (8.0 * (1.0 - POISSON) * distance_sq)
    field = (1.0 - 2.0 * POISSON) * (
        burgers[:, :, None] * along_n[None] + normal[:, :, None] * along_b[None]
    )
    field = field - burgers_normal[None] * unit_dir + 3.0 * unit_dir * (along_b * along_n)[None]
    return jnp.sum(strength[None] * field, axis=1)


def waves(first, count, total, centre):
    steps = first + jnp.arange(count, dtype=jnp.float32)
    return TWO_PI / LATTICE * (centre + (steps - total * 0.5 + 0.5) / QX)


def factor_block(xcosines, xsines, zcosines, zsines, ytable):
    ywidth = ytable.shape[0] // 2
    left_real = (
        zcosines[None, :, :] * xcosines[:, None, :] - zsines[None, :, :] * xsines[:, None, :]
    )
    left_imag = (
        zcosines[None, :, :] * xsines[:, None, :] + zsines[None, :, :] * xcosines[:, None, :]
    )
    left_pair = jnp.stack([left_real, left_imag], axis=2)
    product = jnp.einsum(
        "xzca,da->xzcd",
        left_pair,
        ytable,
        precision=lax.Precision.HIGH,
        preferred_element_type=jnp.float32,
    )
    real_part = product[:, :, 0, :ywidth] - product[:, :, 1, ywidth:]
    imag_part = product[:, :, 0, ywidth:] + product[:, :, 1, :ywidth]
    return jnp.stack([real_part, imag_part], axis=1)


FINE_STEPS = 16


def sincos_rows(coarse, fine, values):
    coarse_angle = coarse[:, None] * values[None, :]
    fine_angle = fine[:, None] * values[None, :]
    cc, sc = jnp.cos(coarse_angle), jnp.sin(coarse_angle)
    cf, sf = jnp.cos(fine_angle), jnp.sin(fine_angle)
    cosines = cc[:, None, :] * cf[None, :, :] - sc[:, None, :] * sf[None, :, :]
    sines = sc[:, None, :] * cf[None, :, :] + cc[:, None, :] * sf[None, :, :]
    shape = (coarse.shape[0] * fine.shape[0], values.shape[0])
    return cosines.reshape(shape), sines.reshape(shape)


def steps_of(waves_row, picked=None):
    fine = waves_row[:FINE_STEPS] - waves_row[0]
    if picked is not None:
        fine = jnp.take(fine, picked)
    return waves_row[::FINE_STEPS], fine


def phase_tables(position, ywaves, zwaves):
    ycosines, ysines = sincos_rows(*steps_of(ywaves), position[1])
    zangle = zwaves[:, None] * position[2][None, :]
    ytable = jnp.concatenate([ycosines, ysines], axis=0)
    return jnp.cos(zangle), jnp.sin(zangle), ytable


HALF_BURGERS = float(BURGERS_TABLE[0, 0])
HABIT_SCALE = float(NORMAL_TABLE[0, 0])
STRENGTH_SCALE = 1.0 / (8.0 * (1.0 - POISSON))
FIELD_SPLIT = 2
FIELD_UNROLL = 2
FIELD_SLOTS = 8


def field_kernel(cells, burgers_index, habit_index, radius, site, anchor_out, field_out):
    whole = site[...]
    basis = jnp.bitwise_and(whole, 1)
    cell = jnp.right_shift(whole, 1)
    first = jnp.bitwise_and(cell, WIN_X - 1)
    second = jnp.bitwise_and(jnp.right_shift(cell, 5), WIN_Y - 1)
    third = jnp.right_shift(cell, 10)
    half = 0.5 * basis.astype(jnp.float32)
    coords = [LATTICE * (c.astype(jnp.float32) + half) for c in (first, second, third)]
    rows = whole.shape[0] // FIELD_SPLIT
    slots = field_out.shape[0] // rows
    spare = jnp.zeros((rows, whole.shape[1]), jnp.float32)
    for p in range(FIELD_SPLIT):
        for axis in range(3):
            piece = coords[axis][p * rows : (p + 1) * rows]
            anchor_out[pl.ds(axis * FIELD_SPLIT + p, rows, stride=slots), :] = piece
    for slot in range(3 * FIELD_SPLIT, slots):
        anchor_out[pl.ds(slot, rows, stride=slots), :] = spare
    pieces = [[c[p * rows : (p + 1) * rows] for c in coords] for p in range(FIELD_SPLIT)]

    def one_loop(number, running):
        cx = LATTICE * (cells[0, number].astype(jnp.float32) + 0.25)
        cy = LATTICE * (cells[1, number].astype(jnp.float32) + 0.25)
        cz = LATTICE * (cells[2, number].astype(jnp.float32) + 0.25)
        kb = burgers_index[number]
        kh = habit_index[number]
        h = jnp.float32(HALF_BURGERS)
        bx = jnp.where(kb == 1, -h, h)
        by = jnp.where(kb == 2, -h, h)
        bz = jnp.where(kb == 3, -h, h)
        c = jnp.float32(HABIT_SCALE)
        zero = jnp.float32(0.0)
        nx = jnp.where(kh < 4, c, zero)
        ny = jnp.where(kh == 1, -c, jnp.where((kh == 2) | (kh == 3), zero, c))
        nz = jnp.where((kh == 2) | (kh == 4), c, jnp.where((kh == 3) | (kh == 5), -c, zero))
        burgers_normal = bx * nx + by * ny + bz * nz
        r = radius[number]
        radius_sq = r * r
        scale = radius_sq * jnp.float32(STRENGTH_SCALE)
        scaled_b = [jnp.float32(1.0 - 2.0 * POISSON) * v for v in (bx, by, bz)]
        scaled_n = [jnp.float32(1.0 - 2.0 * POISSON) * v for v in (nx, ny, nz)]
        out = []
        for p in range(FIELD_SPLIT):
            ax, ay, az = pieces[p]
            dx, dy, dz = ax - cx, ay - cy, az - cz
            distance_sq = dx * dx + dy * dy + dz * dz + radius_sq
            inverse = lax.rsqrt(distance_sq)
            inverse_sq = inverse * inverse
            toward_b = bx * dx + by * dy + bz * dz
            toward_n = nx * dx + ny * dy + nz * dz
            weight = scale * (inverse_sq * inverse)
            mixed = (3.0 * inverse_sq) * (toward_b * toward_n) - burgers_normal
            on_n = weight * toward_n
            on_b = weight * toward_b
            on_d = weight * mixed
            out.append(
                tuple(
                    total + (sb * on_n + sn * on_b + d * on_d)
                    for total, sb, sn, d in zip(running[p], scaled_b, scaled_n, (dx, dy, dz))
                )
            )
        return tuple(out)

    zero = jnp.zeros((rows, whole.shape[1]), jnp.float32)
    start = tuple((zero, zero, zero) for _ in range(FIELD_SPLIT))
    totals = lax.fori_loop(0, radius.shape[0], one_loop, start, unroll=FIELD_UNROLL)
    for p in range(FIELD_SPLIT):
        for axis in range(3):
            field_out[pl.ds(axis * FIELD_SPLIT + p, rows, stride=slots), :] = totals[p][axis]
    for slot in range(3 * FIELD_SPLIT, slots):
        field_out[pl.ds(slot, rows, stride=slots), :] = spare


def anchor_and_field(atom_site, loop_cells, loop_burgers, loop_habit, loop_radius):
    atoms = atom_site.shape[0]
    loops = loop_radius.shape[0]
    tiled = atom_site.reshape(atoms // 128, 128)
    smem = pl.BlockSpec(memory_space=pltpu.SMEM)
    vmem = pl.BlockSpec(memory_space=pltpu.VMEM)
    rows = tiled.shape[0] // FIELD_SPLIT
    chunked = jax.ShapeDtypeStruct((rows * FIELD_SLOTS, 128), jnp.float32)
    anchor, field = pl.pallas_call(
        field_kernel,
        in_specs=[smem, smem, smem, smem, vmem],
        out_specs=[vmem, vmem],
        out_shape=[chunked, chunked],
        cost_estimate=pl.CostEstimate(
            flops=55 * atoms * loops, transcendentals=atoms * loops, bytes_accessed=28 * atoms
        ),
    )(loop_cells, loop_burgers, loop_habit, loop_radius, tiled)
    return anchor, field

def body(atom_site, loop_cells, loop_burgers, loop_habit, loop_radius):
    anchor, field = anchor_and_field(atom_site, loop_cells, loop_burgers, loop_habit, loop_radius)
    loop_groups = lax.axis_size("loops")
    chunks = field.reshape(loop_groups, FIELD_SLOTS, field.shape[1])
    own_anchor = lax.dynamic_index_in_dim(
        anchor.reshape(chunks.shape), lax.axis_index("loops"), axis=0, keepdims=False
    )
    owned = lax.all_to_all(chunks, "loops", 0, 0, tiled=True).sum(axis=0) + own_anchor
    gathered = lax.all_to_all(
        jnp.broadcast_to(owned[None], chunks.shape), "loops", 0, 0, tiled=True
    )
    position = [
        gathered[:, axis * FIELD_SPLIT : (axis + 1) * FIELD_SPLIT].reshape(-1) for axis in range(3)
    ]
    group_count = lax.axis_size((ATOM_OUTER, ATOM_CORE))
    zrows = QZ // lax.axis_size("loops")
    atom_total = position[0].shape[0] * group_count
    zfirst = (lax.axis_index("loops") * zrows).astype(jnp.float32)
    zwaves = waves(zfirst, zrows, QZ, 0.0)
    ywaves = waves(jnp.float32(0.0), QY, QY, 1.0)
    xwaves = waves(jnp.float32(0.0), QX, QX, 1.0)
    zcosines, zsines, ytable = phase_tables(position, ywaves, zwaves)
    outer = lax.axis_size(ATOM_OUTER)
    core = lax.axis_index(ATOM_CORE)
    block = QX // (2 * outer)
    lanes = np.arange(FINE_STEPS)
    first_side = jnp.asarray(lanes[(lanes // block) % 2 == 0], jnp.int32)

    def half(side):
        xcosines, xsines = sincos_rows(*steps_of(xwaves, first_side + block * side), position[0])
        return factor_block(xcosines, xsines, zcosines, zsines, ytable)

    sent = half(1 - core)
    arrived = lax.ppermute(sent, ATOM_CORE, [(0, 1), (1, 0)])
    kept = half(core)
    partial = kept + arrived
    blocks = partial.reshape(outer, -1, *partial.shape[1:])
    summed = lax.all_to_all(blocks, ATOM_OUTER, 0, 0, tiled=True).sum(axis=0)
    power = summed[:, 0] ** 2 + summed[:, 1] ** 2
    return jnp.log1p(jnp.transpose(power, (1, 0, 2)) / atom_total)


ATOM_OUTER = "atom_pairs"
ATOM_CORE = "atom_core"


def solution(mesh):
    groups, loop_groups = mesh.devices.shape
    paired = Mesh(
        mesh.devices.reshape(groups // 2, 2, loop_groups), (ATOM_OUTER, ATOM_CORE, "loops")
    )
    atoms = (ATOM_OUTER, ATOM_CORE)
    placed = (P(atoms), P(None, "loops"), P("loops"), P("loops"), P("loops"))
    return jax.shard_map(
        body, mesh=paired, in_specs=placed, out_specs=P("loops", atoms, None), check_vma=False
    )
```

```python
import math

import jax
import jax.numpy as jnp
import numpy as np
from jax import lax
from jax.experimental import pallas as pl
from jax.experimental.pallas import tpu as pltpu
from jax.sharding import Mesh, PartitionSpec as P

WIN_X = 32
WIN_Y = 32
QX = 128
QY = 128
QZ = 64


LATTICE = 2.8665
POISSON = 0.29
TWO_PI = 2.0 * math.pi
BURGERS_TABLE = np.array(
    [[1.0, 1.0, 1.0], [-1.0, 1.0, 1.0], [1.0, -1.0, 1.0], [1.0, 1.0, -1.0]]
) * (0.5 * LATTICE)
NORMAL_TABLE = (
    np.array(
        [
            [1.0, 1.0, 0.0],
            [1.0, -1.0, 0.0],
            [1.0, 0.0, 1.0],
            [1.0, 0.0, -1.0],
            [0.0, 1.0, 1.0],
            [0.0, 1.0, -1.0],
        ]
    )
    * 0.70710678
)


def lookup(index, table):
    columns = []
    for column in range(3):
        total = jnp.zeros(index.shape, jnp.float32)
        for entry in range(table.shape[0]):
            total = total + jnp.where(
                index == entry, jnp.float32(table[entry, column]), jnp.float32(0.0)
            )
        columns.append(total)
    return jnp.stack(columns)


def site_anchor(site):
    basis = site % 2
    cell = site // 2
    first = cell % WIN_X
    second = cell // WIN_X % WIN_Y
    third = cell // (WIN_X * WIN_Y)
    cells = jnp.stack([first, second, third]).astype(jnp.float32)
    return LATTICE * (cells + 0.5 * basis.astype(jnp.float32)[None, :])


def loop_centre(cells):
    return LATTICE * (cells.astype(jnp.float32) + 0.25)


def loop_field(anchor, centre, burgers, normal, radius):
    offset = anchor[:, None, :] - centre[:, :, None]
    radius_sq = (radius * radius)[:, None]
    distance_sq = jnp.sum(offset * offset, axis=0) + radius_sq
    unit_dir = offset * lax.rsqrt(distance_sq)[None]
    along_b = jnp.sum(burgers[:, :, None] * unit_dir, axis=0)
    along_n = jnp.sum(normal[:, :, None] * unit_dir, axis=0)
    burgers_normal = jnp.sum(burgers * normal, axis=0)[:, None]
    strength = radius_sq / (8.0 * (1.0 - POISSON) * distance_sq)
    field = (1.0 - 2.0 * POISSON) * (
        burgers[:, :, None] * along_n[None] + normal[:, :, None] * along_b[None]
    )
    field = field - burgers_normal[None] * unit_dir + 3.0 * unit_dir * (along_b * along_n)[None]
    return jnp.sum(strength[None] * field, axis=1)


def waves(first, count, total, centre):
    steps = first + jnp.arange(count, dtype=jnp.float32)
    return TWO_PI / LATTICE * (centre + (steps - total * 0.5 + 0.5) / QX)


def factor_block(xcosines, xsines, zcosines, zsines, ytable):
    ywidth = ytable.shape[0] // 2
    left_real = (
        zcosines[None, :, :] * xcosines[:, None, :] - zsines[None, :, :] * xsines[:, None, :]
    )
    left_imag = (
        zcosines[None, :, :] * xsines[:, None, :] + zsines[None, :, :] * xcosines[:, None, :]
    )
    left_pair = jnp.stack([left_real, left_imag], axis=2)
    product = jnp.einsum(
        "xzca,da->xzcd",
        left_pair,
        ytable,
        precision=lax.Precision.HIGH,
        preferred_element_type=jnp.float32,
    )
    real_part = product[:, :, 0, :ywidth] - product[:, :, 1, ywidth:]
    imag_part = product[:, :, 0, ywidth:] + product[:, :, 1, :ywidth]
    return jnp.stack([real_part, imag_part], axis=1)


FINE_STEPS = 16


def sincos_rows(coarse, fine, values):
    coarse_angle = coarse[:, None] * values[None, :]
    fine_angle = fine[:, None] * values[None, :]
    cc, sc = jnp.cos(coarse_angle), jnp.sin(coarse_angle)
    cf, sf = jnp.cos(fine_angle), jnp.sin(fine_angle)
    cosines = cc[:, None, :] * cf[None, :, :] - sc[:, None, :] * sf[None, :, :]
    sines = sc[:, None, :] * cf[None, :, :] + cc[:, None, :] * sf[None, :, :]
    shape = (coarse.shape[0] * fine.shape[0], values.shape[0])
    return cosines.reshape(shape), sines.reshape(shape)


def steps_of(waves_row, picked=None):
    fine = waves_row[:FINE_STEPS] - waves_row[0]
    if picked is not None:
        fine = jnp.take(fine, picked)
    return waves_row[::FINE_STEPS], fine


def phase_tables(position, ywaves, zwaves):
    ycosines, ysines = sincos_rows(*steps_of(ywaves), position[1])
    zangle = zwaves[:, None] * position[2][None, :]
    ytable = jnp.concatenate([ycosines, ysines], axis=0)
    return jnp.cos(zangle), jnp.sin(zangle), ytable


HALF_BURGERS = float(BURGERS_TABLE[0, 0])
HABIT_SCALE = float(NORMAL_TABLE[0, 0])
STRENGTH_SCALE = 1.0 / (8.0 * (1.0 - POISSON))
FIELD_SPLIT = 2
FIELD_UNROLL = 2
FIELD_SLOTS = 8


def field_kernel(cells, burgers_index, habit_index, radius, site, anchor_out, field_out):
    whole = site[...]
    basis = jnp.bitwise_and(whole, 1)
    cell = jnp.right_shift(whole, 1)
    first = jnp.bitwise_and(cell, WIN_X - 1)
    second = jnp.bitwise_and(jnp.right_shift(cell, 5), WIN_Y - 1)
    third = jnp.right_shift(cell, 10)
    half = 0.5 * basis.astype(jnp.float32)
    coords = [LATTICE * (c.astype(jnp.float32) + half) for c in (first, second, third)]
    rows = whole.shape[0] // FIELD_SPLIT
    slots = field_out.shape[0] // rows
    spare = jnp.zeros((rows, whole.shape[1]), jnp.float32)
    for p in range(FIELD_SPLIT):
        for axis in range(3):
            piece = coords[axis][p * rows : (p + 1) * rows]
            anchor_out[pl.ds(axis * FIELD_SPLIT + p, rows, stride=slots), :] = piece
    for slot in range(3 * FIELD_SPLIT, slots):
        anchor_out[pl.ds(slot, rows, stride=slots), :] = spare
    pieces = [[c[p * rows : (p + 1) * rows] for c in coords] for p in range(FIELD_SPLIT)]

    def one_loop(number, running):
        cx = LATTICE * (cells[0, number].astype(jnp.float32) + 0.25)
        cy = LATTICE * (cells[1, number].astype(jnp.float32) + 0.25)
        cz = LATTICE * (cells[2, number].astype(jnp.float32) + 0.25)
        kb = burgers_index[number]
        kh = habit_index[number]
        h = jnp.float32(HALF_BURGERS)
        bx = jnp.where(kb == 1, -h, h)
        by = jnp.where(kb == 2, -h, h)
        bz = jnp.where(kb == 3, -h, h)
        c = jnp.float32(HABIT_SCALE)
        zero = jnp.float32(0.0)
        nx = jnp.where(kh < 4, c, zero)
        ny = jnp.where(kh == 1, -c, jnp.where((kh == 2) | (kh == 3), zero, c))
        nz = jnp.where((kh == 2) | (kh == 4), c, jnp.where((kh == 3) | (kh == 5), -c, zero))
        burgers_normal = bx * nx + by * ny + bz * nz
        r = radius[number]
        radius_sq = r * r
        scale = radius_sq * jnp.float32(STRENGTH_SCALE)
        scaled_b = [jnp.float32(1.0 - 2.0 * POISSON) * v for v in (bx, by, bz)]
        scaled_n = [jnp.float32(1.0 - 2.0 * POISSON) * v for v in (nx, ny, nz)]
        out = []
        for p in range(FIELD_SPLIT):
            ax, ay, az = pieces[p]
            dx, dy, dz = ax - cx, ay - cy, az - cz
            distance_sq = dx * dx + dy * dy + dz * dz + radius_sq
            inverse = lax.rsqrt(distance_sq)
            inverse_sq = inverse * inverse
            toward_b = bx * dx + by * dy + bz * dz
            toward_n = nx * dx + ny * dy + nz * dz
            weight = scale * (inverse_sq * inverse)
            mixed = (3.0 * inverse_sq) * (toward_b * toward_n) - burgers_normal
            on_n = weight * toward_n
            on_b = weight * toward_b
            on_d = weight * mixed
            out.append(
                tuple(
                    total + (sb * on_n + sn * on_b + d * on_d)
                    for total, sb, sn, d in zip(running[p], scaled_b, scaled_n, (dx, dy, dz))
                )
            )
        return tuple(out)

    zero = jnp.zeros((rows, whole.shape[1]), jnp.float32)
    start = tuple((zero, zero, zero) for _ in range(FIELD_SPLIT))
    totals = lax.fori_loop(0, radius.shape[0], one_loop, start, unroll=FIELD_UNROLL)
    for p in range(FIELD_SPLIT):
        for axis in range(3):
            field_out[pl.ds(axis * FIELD_SPLIT + p, rows, stride=slots), :] = totals[p][axis]
    for slot in range(3 * FIELD_SPLIT, slots):
        field_out[pl.ds(slot, rows, stride=slots), :] = spare


def anchor_and_field(atom_site, loop_cells, loop_burgers, loop_habit, loop_radius):
    atoms = atom_site.shape[0]
    loops = loop_radius.shape[0]
    tiled = atom_site.reshape(atoms // 128, 128)
    smem = pl.BlockSpec(memory_space=pltpu.SMEM)
    vmem = pl.BlockSpec(memory_space=pltpu.VMEM)
    rows = tiled.shape[0] // FIELD_SPLIT
    chunked = jax.ShapeDtypeStruct((rows * FIELD_SLOTS, 128), jnp.float32)
    anchor, field = pl.pallas_call(
        field_kernel,
        in_specs=[smem, smem, smem, smem, vmem],
        out_specs=[vmem, vmem],
        out_shape=[chunked, chunked],
        cost_estimate=pl.CostEstimate(
            flops=55 * atoms * loops, transcendentals=atoms * loops, bytes_accessed=28 * atoms
        ),
    )(loop_cells, loop_burgers, loop_habit, loop_radius, tiled)
    return anchor, field

def body(atom_site, loop_cells, loop_burgers, loop_habit, loop_radius):
    anchor, field = anchor_and_field(atom_site, loop_cells, loop_burgers, loop_habit, loop_radius)
    loop_groups = lax.axis_size("loops")
    chunks = field.reshape(loop_groups, FIELD_SLOTS, field.shape[1])
    own_anchor = lax.dynamic_index_in_dim(
        anchor.reshape(chunks.shape), lax.axis_index("loops"), axis=0, keepdims=False
    )
    owned = lax.all_to_all(chunks, "loops", 0, 0, tiled=True).sum(axis=0) + own_anchor
    gathered = lax.all_to_all(
        jnp.broadcast_to(owned[None], chunks.shape), "loops", 0, 0, tiled=True
    )
    position = [
        gathered[:, axis * FIELD_SPLIT : (axis + 1) * FIELD_SPLIT].reshape(-1) for axis in range(3)
    ]
    group_count = lax.axis_size((ATOM_HALF, ATOM_INNER))
    zrows = QZ // lax.axis_size("loops")
    atom_total = position[0].shape[0] * group_count
    zfirst = (lax.axis_index("loops") * zrows).astype(jnp.float32)
    zwaves = waves(zfirst, zrows, QZ, 0.0)
    ywaves = waves(jnp.float32(0.0), QY, QY, 1.0)
    xwaves = waves(jnp.float32(0.0), QX, QX, 1.0)
    zcosines, zsines, ytable = phase_tables(position, ywaves, zwaves)
    inner = lax.axis_size(ATOM_INNER)
    side = lax.axis_index(ATOM_HALF)
    xcoarse, xfine = steps_of(xwaves)
    width = xcoarse.shape[0] // 2

    def half(part):
        coarse = lax.dynamic_slice_in_dim(xcoarse, part * width, width)
        xcosines, xsines = sincos_rows(coarse, xfine, position[0])
        return factor_block(xcosines, xsines, zcosines, zsines, ytable)

    sent = half(1 - side)
    arrived = lax.ppermute(sent, ATOM_HALF, [(0, 1), (1, 0)])
    kept = half(side)
    partial = kept + arrived
    blocks = partial.reshape(inner, -1, *partial.shape[1:])
    summed = lax.all_to_all(blocks, ATOM_INNER, 0, 0, tiled=True).sum(axis=0)
    power = summed[:, 0] ** 2 + summed[:, 1] ** 2
    return jnp.log1p(jnp.transpose(power, (1, 0, 2)) / atom_total)


ATOM_HALF = "atom_half"
ATOM_INNER = "atom_inner"


def solution(mesh):
    groups, loop_groups = mesh.devices.shape
    halves = Mesh(mesh.devices.reshape(2, groups // 2, loop_groups), (ATOM_HALF, ATOM_INNER, "loops"))
    atoms = (ATOM_HALF, ATOM_INNER)
    placed = (P(atoms), P(None, "loops"), P("loops"), P("loops"), P("loops"))
    return jax.shard_map(
        body, mesh=halves, in_specs=placed, out_specs=P("loops", atoms, None), check_vma=False
    )
```

```python
import math

import jax
import jax.numpy as jnp
import numpy as np
from jax import lax
from jax.experimental import pallas as pl
from jax.experimental.pallas import tpu as pltpu
from jax.sharding import Mesh, PartitionSpec as P

WIN_X = 32
WIN_Y = 32
QX = 128
QY = 128
QZ = 64


LATTICE = 2.8665
POISSON = 0.29
TWO_PI = 2.0 * math.pi
BURGERS_TABLE = np.array(
    [[1.0, 1.0, 1.0], [-1.0, 1.0, 1.0], [1.0, -1.0, 1.0], [1.0, 1.0, -1.0]]
) * (0.5 * LATTICE)
NORMAL_TABLE = (
    np.array(
        [
            [1.0, 1.0, 0.0],
            [1.0, -1.0, 0.0],
            [1.0, 0.0, 1.0],
            [1.0, 0.0, -1.0],
            [0.0, 1.0, 1.0],
            [0.0, 1.0, -1.0],
        ]
    )
    * 0.70710678
)


def lookup(index, table):
    columns = []
    for column in range(3):
        total = jnp.zeros(index.shape, jnp.float32)
        for entry in range(table.shape[0]):
            total = total + jnp.where(
                index == entry, jnp.float32(table[entry, column]), jnp.float32(0.0)
            )
        columns.append(total)
    return jnp.stack(columns)


def site_anchor(site):
    basis = site % 2
    cell = site // 2
    first = cell % WIN_X
    second = cell // WIN_X % WIN_Y
    third = cell // (WIN_X * WIN_Y)
    cells = jnp.stack([first, second, third]).astype(jnp.float32)
    return LATTICE * (cells + 0.5 * basis.astype(jnp.float32)[None, :])


def loop_centre(cells):
    return LATTICE * (cells.astype(jnp.float32) + 0.25)


def loop_field(anchor, centre, burgers, normal, radius):
    offset = anchor[:, None, :] - centre[:, :, None]
    radius_sq = (radius * radius)[:, None]
    distance_sq = jnp.sum(offset * offset, axis=0) + radius_sq
    unit_dir = offset * lax.rsqrt(distance_sq)[None]
    along_b = jnp.sum(burgers[:, :, None] * unit_dir, axis=0)
    along_n = jnp.sum(normal[:, :, None] * unit_dir, axis=0)
    burgers_normal = jnp.sum(burgers * normal, axis=0)[:, None]
    strength = radius_sq / (8.0 * (1.0 - POISSON) * distance_sq)
    field = (1.0 - 2.0 * POISSON) * (
        burgers[:, :, None] * along_n[None] + normal[:, :, None] * along_b[None]
    )
    field = field - burgers_normal[None] * unit_dir + 3.0 * unit_dir * (along_b * along_n)[None]
    return jnp.sum(strength[None] * field, axis=1)


def waves(first, count, total, centre):
    steps = first + jnp.arange(count, dtype=jnp.float32)
    return TWO_PI / LATTICE * (centre + (steps - total * 0.5 + 0.5) / QX)


def factor_block(xcosines, xsines, zcosines, zsines, ytable):
    ywidth = ytable.shape[0] // 2
    left_real = (
        zcosines[None, :, :] * xcosines[:, None, :] - zsines[None, :, :] * xsines[:, None, :]
    )
    left_imag = (
        zcosines[None, :, :] * xsines[:, None, :] + zsines[None, :, :] * xcosines[:, None, :]
    )
    left_pair = jnp.stack([left_real, left_imag], axis=2)
    product = jnp.einsum(
        "xzca,da->xzcd",
        left_pair,
        ytable,
        precision=lax.Precision.HIGH,
        preferred_element_type=jnp.float32,
    )
    real_part = product[:, :, 0, :ywidth] - product[:, :, 1, ywidth:]
    imag_part = product[:, :, 0, ywidth:] + product[:, :, 1, :ywidth]
    return jnp.stack([real_part, imag_part], axis=1)


FINE_STEPS = 16


def sincos_rows(coarse, fine, values):
    coarse_angle = coarse[:, None] * values[None, :]
    fine_angle = fine[:, None] * values[None, :]
    cc, sc = jnp.cos(coarse_angle), jnp.sin(coarse_angle)
    cf, sf = jnp.cos(fine_angle), jnp.sin(fine_angle)
    cosines = cc[:, None, :] * cf[None, :, :] - sc[:, None, :] * sf[None, :, :]
    sines = sc[:, None, :] * cf[None, :, :] + cc[:, None, :] * sf[None, :, :]
    shape = (coarse.shape[0] * fine.shape[0], values.shape[0])
    return cosines.reshape(shape), sines.reshape(shape)


def steps_of(waves_row, picked=None):
    fine = waves_row[:FINE_STEPS] - waves_row[0]
    if picked is not None:
        fine = jnp.take(fine, picked)
    return waves_row[::FINE_STEPS], fine


def phase_tables(position, ywaves, zwaves):
    ycosines, ysines = sincos_rows(*steps_of(ywaves), position[1])
    zangle = zwaves[:, None] * position[2][None, :]
    ytable = jnp.concatenate([ycosines, ysines], axis=0)
    return jnp.cos(zangle), jnp.sin(zangle), ytable


HALF_BURGERS = float(BURGERS_TABLE[0, 0])
HABIT_SCALE = float(NORMAL_TABLE[0, 0])
STRENGTH_SCALE = 1.0 / (8.0 * (1.0 - POISSON))
FIELD_SPLIT = 2
FIELD_UNROLL = 2
FIELD_SLOTS = 8


def field_kernel(owner, cells, burgers_index, habit_index, radius, site, field_out):
    whole = site[...]
    basis = jnp.bitwise_and(whole, 1)
    cell = jnp.right_shift(whole, 1)
    first = jnp.bitwise_and(cell, WIN_X - 1)
    second = jnp.bitwise_and(jnp.right_shift(cell, 5), WIN_Y - 1)
    third = jnp.right_shift(cell, 10)
    half = 0.5 * basis.astype(jnp.float32)
    coords = [LATTICE * (c.astype(jnp.float32) + half) for c in (first, second, third)]
    rows = whole.shape[0] // FIELD_SPLIT
    slots = field_out.shape[0] // rows
    spare = jnp.zeros((rows, whole.shape[1]), jnp.float32)
    pieces = [[c[p * rows : (p + 1) * rows] for c in coords] for p in range(FIELD_SPLIT)]

    def one_loop(number, running):
        cx = LATTICE * (cells[0, number].astype(jnp.float32) + 0.25)
        cy = LATTICE * (cells[1, number].astype(jnp.float32) + 0.25)
        cz = LATTICE * (cells[2, number].astype(jnp.float32) + 0.25)
        kb = burgers_index[number]
        kh = habit_index[number]
        h = jnp.float32(HALF_BURGERS)
        bx = jnp.where(kb == 1, -h, h)
        by = jnp.where(kb == 2, -h, h)
        bz = jnp.where(kb == 3, -h, h)
        c = jnp.float32(HABIT_SCALE)
        zero = jnp.float32(0.0)
        nx = jnp.where(kh < 4, c, zero)
        ny = jnp.where(kh == 1, -c, jnp.where((kh == 2) | (kh == 3), zero, c))
        nz = jnp.where((kh == 2) | (kh == 4), c, jnp.where((kh == 3) | (kh == 5), -c, zero))
        burgers_normal = bx * nx + by * ny + bz * nz
        r = radius[number]
        radius_sq = r * r
        scale = radius_sq * jnp.float32(STRENGTH_SCALE)
        scaled_b = [jnp.float32(1.0 - 2.0 * POISSON) * v for v in (bx, by, bz)]
        scaled_n = [jnp.float32(1.0 - 2.0 * POISSON) * v for v in (nx, ny, nz)]
        out = []
        for p in range(FIELD_SPLIT):
            ax, ay, az = pieces[p]
            dx, dy, dz = ax - cx, ay - cy, az - cz
            distance_sq = dx * dx + dy * dy + dz * dz + radius_sq
            inverse = lax.rsqrt(distance_sq)
            inverse_sq = inverse * inverse
            toward_b = bx * dx + by * dy + bz * dz
            toward_n = nx * dx + ny * dy + nz * dz
            weight = scale * (inverse_sq * inverse)
            mixed = (3.0 * inverse_sq) * (toward_b * toward_n) - burgers_normal
            on_n = weight * toward_n
            on_b = weight * toward_b
            on_d = weight * mixed
            out.append(
                tuple(
                    total + (sb * on_n + sn * on_b + d * on_d)
                    for total, sb, sn, d in zip(running[p], scaled_b, scaled_n, (dx, dy, dz))
                )
            )
        return tuple(out)

    zero = jnp.zeros((rows, whole.shape[1]), jnp.float32)
    start = tuple((zero, zero, zero) for _ in range(FIELD_SPLIT))
    totals = lax.fori_loop(0, radius.shape[0], one_loop, start, unroll=FIELD_UNROLL)
    mine = lax.broadcasted_iota(jnp.int32, spare.shape, 0) == owner[0]
    for p in range(FIELD_SPLIT):
        for axis in range(3):
            total = totals[p][axis] + jnp.where(mine, pieces[p][axis], spare)
            field_out[pl.ds(axis * FIELD_SPLIT + p, rows, stride=slots), :] = total
    for slot in range(3 * FIELD_SPLIT, slots):
        field_out[pl.ds(slot, rows, stride=slots), :] = spare


def anchor_and_field(atom_site, loop_cells, loop_burgers, loop_habit, loop_radius):
    atoms = atom_site.shape[0]
    loops = loop_radius.shape[0]
    tiled = atom_site.reshape(atoms // 128, 128)
    smem = pl.BlockSpec(memory_space=pltpu.SMEM)
    vmem = pl.BlockSpec(memory_space=pltpu.VMEM)
    rows = tiled.shape[0] // FIELD_SPLIT
    chunked = jax.ShapeDtypeStruct((rows * FIELD_SLOTS, 128), jnp.float32)
    owner = lax.axis_index("loops").astype(jnp.int32).reshape(1)
    field = pl.pallas_call(
        field_kernel,
        in_specs=[smem, smem, smem, smem, smem, vmem],
        out_specs=vmem,
        out_shape=chunked,
        cost_estimate=pl.CostEstimate(
            flops=55 * atoms * loops, transcendentals=atoms * loops, bytes_accessed=28 * atoms
        ),
    )(owner, loop_cells, loop_burgers, loop_habit, loop_radius, tiled)
    return field

def body(atom_site, loop_cells, loop_burgers, loop_habit, loop_radius):
    field = anchor_and_field(atom_site, loop_cells, loop_burgers, loop_habit, loop_radius)
    loop_groups = lax.axis_size("loops")
    chunks = field.reshape(loop_groups, FIELD_SLOTS, field.shape[1])
    owned = lax.all_to_all(chunks, "loops", 0, 0, tiled=True).sum(axis=0)
    gathered = lax.all_to_all(
        jnp.broadcast_to(owned[None], chunks.shape), "loops", 0, 0, tiled=True
    )
    position = [
        gathered[:, axis * FIELD_SPLIT : (axis + 1) * FIELD_SPLIT].reshape(-1) for axis in range(3)
    ]
    group_count = lax.axis_size((ATOM_OUTER, ATOM_CORE))
    zrows = QZ // lax.axis_size("loops")
    atom_total = position[0].shape[0] * group_count
    zfirst = (lax.axis_index("loops") * zrows).astype(jnp.float32)
    zwaves = waves(zfirst, zrows, QZ, 0.0)
    ywaves = waves(jnp.float32(0.0), QY, QY, 1.0)
    xwaves = waves(jnp.float32(0.0), QX, QX, 1.0)
    zcosines, zsines, ytable = phase_tables(position, ywaves, zwaves)
    outer = lax.axis_size(ATOM_OUTER)
    core = lax.axis_index(ATOM_CORE)
    block = QX // (2 * outer)
    lanes = np.arange(FINE_STEPS)
    first_side = jnp.asarray(lanes[(lanes // block) % 2 == 0], jnp.int32)

    def half(side):
        xcosines, xsines = sincos_rows(*steps_of(xwaves, first_side + block * side), position[0])
        return factor_block(xcosines, xsines, zcosines, zsines, ytable)

    sent = half(1 - core)
    arrived = lax.ppermute(sent, ATOM_CORE, [(0, 1), (1, 0)])
    kept = half(core)
    partial = kept + arrived
    blocks = partial.reshape(outer, -1, *partial.shape[1:])
    summed = lax.all_to_all(blocks, ATOM_OUTER, 0, 0, tiled=True).sum(axis=0)
    power = summed[:, 0] ** 2 + summed[:, 1] ** 2
    return jnp.log1p(jnp.transpose(power, (1, 0, 2)) / atom_total)


ATOM_OUTER = "atom_pairs"
ATOM_CORE = "atom_core"


def solution(mesh):
    groups, loop_groups = mesh.devices.shape
    paired = Mesh(
        mesh.devices.reshape(groups // 2, 2, loop_groups), (ATOM_OUTER, ATOM_CORE, "loops")
    )
    atoms = (ATOM_OUTER, ATOM_CORE)
    placed = (P(atoms), P(None, "loops"), P("loops"), P("loops"), P("loops"))
    return jax.shard_map(
        body, mesh=paired, in_specs=placed, out_specs=P("loops", atoms, None), check_vma=False
    )
```
